128 devices in a mesh: fsdp: 32 (over z, y, core), fac: 4 (over x).
Axes of the slice: x: 4, y: 4, z: 4, core: 2. Of those that a mesh axis runs over, the one named last changes fastest.
Arguments:
- activations: bfloat16 [32768, 3072], P('fsdp'), may hold values from -6 to 6
- out_grads: bfloat16 [32768, 3072], P('fsdp', 'fac'), may hold values from -12 to 12
- token_ids: int32 [32768], P('fsdp'), may hold values from 0 to 32767
- forget_mask: int32 [32768], P('fsdp'), may hold values 0 or 1
- importance: float32 [32768], replicated, may hold values from 0.3 to 3
- in_inverse: bfloat16 [3072, 3072], P('fsdp'), may hold values from -1 to 3, as said below
- out_inverse: bfloat16 [3072, 3072], P(None, 'fac'), may hold values from -1 to 3, as said below
Outputs:
- newton_step: float32 [3072, 3072], P('fsdp', 'fac')
- residual: float32 [3072, 3072], P('fsdp', 'fac')
The draws below stay inside these ranges and needn't reach their ends.
Inputs may be any that keep to these rules, and one draw needn't show every extreme that they name: `in_inverse`: symmetric and positive definite. `out_inverse`: symmetric and positive definite.
All inputs are finite; a program needn't handle non-finite values. No bound on the sum of `forget_mask` on one device may be relied on, other than what follows from the above.
Results may differ from the reference program's by a relative error of at most 0.03.
Values may be sent and summed in bfloat16 or wider, within the bound.
No kernel may reach another device: no remote copies, remote signals or barrier semaphores. Data moves between devices by JAX's collectives and lax.ppermute only.
A program may use at most 64 MiB of HBM per device.

```python
import math
import jax
import jax.numpy as jnp
import numpy as np
from jax import lax

D_IN = 3072
D_OUT = 3072
VOCAB = 32768
TOK_DEV = 1024
ITERS = 2
TOKENS = 32768
N_FSDP = 32


def symmetric_inverse(key, matrix_order):
    key_noise, key_diag = jax.random.split(key)
    noise_part = jax.random.normal(key_noise, (matrix_order, matrix_order), jnp.float32)
    diag_part = jnp.exp(jax.random.uniform(key_diag, (matrix_order,), jnp.float32, math.log(0.8), math.log(2.0)))
    spread_scale = 0.22 / math.sqrt(matrix_order)
    return jnp.diag(diag_part) + spread_scale * (noise_part + noise_part.T)


def draw_in_inverse(key, part):
    return symmetric_inverse(jax.random.fold_in(key, 11), D_IN).astype(jnp.bfloat16)


def draw_out_inverse(key, part):
    return symmetric_inverse(jax.random.fold_in(key, 23), D_OUT).astype(jnp.bfloat16)


def touch_ends(entries, key, least, largest):
    extent = entries.shape
    place = [jax.random.randint(jax.random.fold_in(key, axis), (), 0, extent[axis]) for axis in range(len(extent))]
    entries = entries.at[tuple(place)].set(least)
    longest = extent.index(max(extent))
    place[longest] = (place[longest] + 1) % extent[longest]
    return entries.at[tuple(place)].set(largest)


def block_levels(key, extent, cuts, least, high):
    def one(position, blocks):
        heights = jax.random.uniform(jax.random.fold_in(jax.random.fold_in(key, 6), position), (blocks,), jnp.float32, least / len(cuts), high / len(cuts))
        return jnp.repeat(jnp.exp(heights), extent[position] // blocks).reshape((-1,) + (1,) * (len(extent) - position - 1))

    loudness = one(*cuts[0])
    for cut in cuts[1:]:
        loudness = loudness * one(*cut)
    return loudness


def cumulative_ranks(number_of, lean):
    portions = [(1 << 20) // math.isqrt(rank ** lean) + 1 for rank in range(1, number_of + 1)]
    width = 1 + sum(portions) // (1 << 30)
    return np.cumsum(np.array([max(1, weight // width) for weight in portions]))


def ranked_ids(own_key, dims, amount, slope):
    listing = cumulative_ranks(amount, slope)
    ticket = jax.random.randint(jax.random.fold_in(own_key, 1), dims, 0, int(listing[amount - 1]))
    rank = jnp.searchsorted(jnp.asarray(listing, jnp.int32), ticket, side="right")
    return jax.random.permutation(jax.random.fold_in(own_key, 2), amount)[rank].astype(jnp.int32)


def gaussian(stream_key, extent, spread, bound, cuts=(), kind=jnp.bfloat16):
    values = jax.random.normal(stream_key, extent, jnp.float32) * spread
    if len(cuts) > 0:
        values = block_levels(stream_key, extent, cuts, -0.22, 0.18) * values
    return jnp.clip(values, min=-bound, max=bound).astype(kind)


def setup_inputs(seed: int = 0) -> dict:
    splits = jax.random.split(jax.random.key(seed), 8)
    return {
        "activations": gaussian(splits[0], (TOKENS, D_IN), 1.0, 6.0, ((0, 32),)),
        "out_grads": gaussian(splits[1], (TOKENS, D_OUT), 2.0, 12.0, ((0, 32), (1, 4))),
        "token_ids": touch_ends(ranked_ids(splits[2], (TOKENS,), VOCAB, 2), jax.random.fold_in(splits[2], 3), 0, VOCAB - 1).astype(jnp.int32),
        "forget_mask": touch_ends((jax.random.randint(splits[3], (TOKENS,), 0, 8) < 1).astype(jnp.int32), jax.random.fold_in(splits[3], 1), 0, 1),
        "importance": jnp.clip(jnp.exp(jax.random.uniform(splits[4], (VOCAB,), jnp.float32, math.log(0.3), math.log(3.0))), 0.3, 3.0),
        "in_inverse": draw_in_inverse(jax.random.fold_in(splits[7], 71), 0),
        "out_inverse": draw_out_inverse(jax.random.fold_in(splits[7], 71), 0),
    }


damping = 0.3

def group_sum(left_groups, right_groups, factor):

    def add_group(carry, pair):
        term = lax.dot_general(pair[0], pair[1], (((0,), (0,)), ((), ())), preferred_element_type=jnp.float32) * factor
        rounded = lax.optimization_barrier(term.astype(jnp.bfloat16))
        return (carry + rounded.astype(jnp.float32), None)
    start_sum = jnp.zeros((left_groups.shape[2], right_groups.shape[2]), jnp.float32)
    summed, unused = lax.scan(add_group, start_sum, (left_groups, right_groups))
    return summed

def reference(activations, out_grads, token_ids, forget_mask, importance, in_inverse, out_inverse):
    keep = 1.0 - forget_mask.astype(jnp.float32)
    weights = importance[token_ids] * keep / TOKENS
    forget_grads = out_grads * forget_mask.astype(jnp.bfloat16)[:, None]
    grouped_acts = activations.reshape(N_FSDP, TOK_DEV, D_IN)
    gradient = group_sum(grouped_acts, forget_grads.reshape(N_FSDP, TOK_DEV, D_OUT), 1.0 / math.sqrt(TOKENS))

    def precondition(matrix):
        mixed = jnp.dot(in_inverse, matrix.astype(jnp.bfloat16), preferred_element_type=jnp.float32)
        return jnp.dot(mixed.astype(jnp.bfloat16), out_inverse, preferred_element_type=jnp.float32)

    def curvature(matrix):
        tok_out = jnp.dot(activations, matrix.astype(jnp.bfloat16), preferred_element_type=jnp.float32)
        scaled = (tok_out * weights[:, None]).astype(jnp.bfloat16)
        return group_sum(grouped_acts, scaled.reshape(N_FSDP, TOK_DEV, D_OUT), 1.0) + damping * matrix
    newton_step = jnp.zeros((D_IN, D_OUT), jnp.float32)
    residual = -gradient
    precond = precondition(residual)
    direction = precond
    inner_now = jnp.sum(residual * precond)
    for iteration in range(ITERS):
        image = curvature(direction)
        alpha = inner_now / jnp.sum(direction * image)
        newton_step = newton_step + alpha * direction
        residual = residual - alpha * image
        if iteration + 1 < ITERS:
            precond = precondition(residual)
            inner_next = jnp.sum(residual * precond)
            direction = precond + inner_next / inner_now * direction
            inner_now = inner_next
    return (newton_step, residual)
```

```python
import math

import jax
import jax.numpy as jnp
from jax import lax
from jax.sharding import PartitionSpec as P

ITERS = 2


damping = 0.3


def add_columns(matrix, piece):
    return jnp.dot(matrix, piece, preferred_element_type=jnp.float32)


def transposed_term(matrix, right):
    return lax.dot_general(
        matrix, right, (((0,), (0,)), ((), ())), preferred_element_type=jnp.float32
    )


def scatter_sum(partial):
    parts = lax.axis_size("fsdp")
    blocks = partial.reshape(parts, partial.shape[0] // parts, partial.shape[1])
    received = lax.all_to_all(blocks, "fsdp", 0, 0, tiled=False)
    return jnp.sum(received.astype(jnp.float32), axis=0)


def global_sums(*partials):
    devices = lax.axis_size("fsdp") * lax.axis_size("fac")
    stacked = jnp.broadcast_to(jnp.stack(partials)[None, :], (devices, len(partials)))
    received = lax.all_to_all(stacked, ("fsdp", "fac"), 0, 0, tiled=True)
    total = jnp.sum(received, axis=0)
    return tuple(total[i] for i in range(len(partials)))


def body(activations, out_grads, token_ids, forget_mask, importance, in_inverse, out_inverse):
    tok_rows = activations.shape[0]
    total = tok_rows * lax.axis_size("fsdp")
    keep = 1.0 - forget_mask.astype(jnp.float32)
    weights = importance[token_ids] * keep / total
    forget_grads = out_grads * forget_mask.astype(jnp.bfloat16)[:, None]
    grad_scale = 1.0 / math.sqrt(total)
    gradient = scatter_sum(
        (transposed_term(activations, forget_grads) * grad_scale).astype(jnp.bfloat16)
    )

    def precondition(matrix):
        matrix_low = matrix.astype(jnp.bfloat16)
        mixed = add_columns(in_inverse, lax.all_gather(matrix_low, "fsdp", axis=0, tiled=True))
        mixed_low = mixed.astype(jnp.bfloat16)
        return jnp.dot(
            lax.all_gather(mixed_low, "fac", axis=1, tiled=True),
            out_inverse,
            preferred_element_type=jnp.float32,
        )

    def inner_part(left, right):
        return jnp.sum(left * right)

    newton_step = jnp.zeros(gradient.shape, jnp.float32)
    residual = -gradient
    precond = precondition(residual)
    direction = precond
    inner_part_now = inner_part(residual, precond)
    for iteration in range(ITERS):
        curvature_matrix_low = direction.astype(jnp.bfloat16)
        tok_out = add_columns(
            activations, lax.all_gather(curvature_matrix_low, "fsdp", axis=0, tiled=True)
        )
        scaled = (tok_out * weights[:, None]).astype(jnp.bfloat16)
        image = (
            scatter_sum(transposed_term(activations, scaled).astype(jnp.bfloat16))
            + damping * direction
        )
        if iteration == 0:
            inner_now, energy = global_sums(inner_part_now, inner_part(direction, image))
        else:
            (energy,) = global_sums(inner_part(direction, image))
        alpha = inner_now / energy
        newton_step = newton_step + alpha * direction
        residual = residual - alpha * image
        if iteration + 1 < ITERS:
            precond = precondition(residual)
            (inner_next,) = global_sums(inner_part(residual, precond))
            direction = precond + inner_next / inner_now * direction
            inner_now = inner_next
    return (newton_step, residual)


def solution(mesh):
    placed = (
        P("fsdp", None),
        P("fsdp", "fac"),
        P("fsdp"),
        P("fsdp"),
        P(),
        P("fsdp", None),
        P(None, "fac"),
    )
    return jax.shard_map(
        body,
        mesh=mesh,
        in_specs=placed,
        out_specs=(P("fsdp", "fac"), P("fsdp", "fac")),
        check_vma=False,
    )
```

```python
import math

import jax
import jax.numpy as jnp
from jax import lax
from jax.sharding import PartitionSpec as P

ITERS = 2


damping = 0.3


def add_columns(matrix, piece):
    return jnp.dot(matrix, piece, preferred_element_type=jnp.float32)


def transposed_term(matrix, right):
    return lax.dot_general(
        matrix, right, (((0,), (0,)), ((), ())), preferred_element_type=jnp.float32
    )


def scatter_sum(partial):
    parts = lax.axis_size("fsdp")
    blocks = partial.reshape(parts, partial.shape[0] // parts, partial.shape[1])
    received = lax.all_to_all(blocks, "fsdp", 0, 0, tiled=False)
    return jnp.sum(received.astype(jnp.float32), axis=0)


def global_sums(*partials):
    devices = lax.axis_size("fsdp") * lax.axis_size("fac")
    stacked = jnp.broadcast_to(jnp.stack(partials)[None, :], (devices, len(partials)))
    received = lax.all_to_all(stacked, ("fsdp", "fac"), 0, 0, tiled=True)
    total = jnp.sum(received, axis=0)
    return tuple(total[i] for i in range(len(partials)))


def body(activations, out_grads, token_ids, forget_mask, importance, in_inverse, out_inverse):
    tok_rows, d_in = activations.shape
    total = tok_rows * lax.axis_size("fsdp")
    keep = 1.0 - forget_mask.astype(jnp.float32)
    weights = importance[token_ids] * keep / total
    forget_grads = out_grads * forget_mask.astype(jnp.bfloat16)[:, None]
    grad_scale = 1.0 / math.sqrt(total)
    d_out_part = out_grads.shape[1]

    gram_cols = d_in // lax.axis_size("fac")
    own_cols = lax.dynamic_slice_in_dim(
        activations, lax.axis_index("fac") * gram_cols, gram_cols, axis=1
    )
    weighted = (own_cols * weights[:, None]).astype(jnp.bfloat16)
    grad_part = (transposed_term(activations, forget_grads) * grad_scale).astype(jnp.bfloat16)
    gram_part = transposed_term(activations, weighted).astype(jnp.bfloat16)
    summed = scatter_sum(jnp.concatenate([grad_part, gram_part], axis=1))
    gradient = summed[:, :d_out_part]
    gram_rows = lax.all_gather(
        summed[:, d_out_part:].astype(jnp.bfloat16), "fac", axis=1, tiled=True
    )

    def precondition(matrix):
        matrix_low = matrix.astype(jnp.bfloat16)
        mixed = add_columns(in_inverse, lax.all_gather(matrix_low, "fsdp", axis=0, tiled=True))
        mixed_low = mixed.astype(jnp.bfloat16)
        return jnp.dot(
            lax.all_gather(mixed_low, "fac", axis=1, tiled=True),
            out_inverse,
            preferred_element_type=jnp.float32,
        )

    def curvature(matrix):
        matrix_low = matrix.astype(jnp.bfloat16)
        gathered = lax.all_gather(matrix_low, "fsdp", axis=0, tiled=True)
        return add_columns(gram_rows, gathered) + damping * matrix

    def inner_part(left, right):
        return jnp.sum(left * right)

    newton_step = jnp.zeros(gradient.shape, jnp.float32)
    residual = -gradient
    precond = precondition(residual)
    direction = precond
    inner_part_now = inner_part(residual, precond)
    for iteration in range(ITERS):
        image = curvature(direction)
        if iteration == 0:
            inner_now, energy = global_sums(inner_part_now, inner_part(direction, image))
        else:
            (energy,) = global_sums(inner_part(direction, image))
        alpha = inner_now / energy
        newton_step = newton_step + alpha * direction
        residual = residual - alpha * image
        if iteration + 1 < ITERS:
            precond = precondition(residual)
            (inner_next,) = global_sums(inner_part(residual, precond))
            direction = precond + inner_next / inner_now * direction
            inner_now = inner_next
    return (newton_step, residual)


def solution(mesh):
    placed = (
        P("fsdp", None),
        P("fsdp", "fac"),
        P("fsdp"),
        P("fsdp"),
        P(),
        P("fsdp", None),
        P(None, "fac"),
    )
    return jax.shard_map(
        body,
        mesh=mesh,
        in_specs=placed,
        out_specs=(P("fsdp", "fac"), P("fsdp", "fac")),
        check_vma=False,
    )
```

```python
import math

import jax
import jax.numpy as jnp
from jax import lax
from jax.sharding import PartitionSpec as P

ITERS = 2


damping = 0.3


def add_columns(matrix, piece):
    return jnp.dot(matrix, piece, preferred_element_type=jnp.float32)


def transposed_term(matrix, right):
    return lax.dot_general(
        matrix, right, (((0,), (0,)), ((), ())), preferred_element_type=jnp.float32
    )


def scatter_sum(partial):
    parts = lax.axis_size("fsdp")
    blocks = partial.reshape(parts, partial.shape[0] // parts, partial.shape[1])
    received = lax.all_to_all(blocks, "fsdp", 0, 0, tiled=False)
    return jnp.sum(received.astype(jnp.float32), axis=0)


def global_sums(*partials):
    devices = lax.axis_size("fsdp") * lax.axis_size("fac")
    stacked = jnp.broadcast_to(jnp.stack(partials)[None, :], (devices, len(partials)))
    received = lax.all_to_all(stacked, ("fsdp", "fac"), 0, 0, tiled=True)
    total = jnp.sum(received, axis=0)
    return tuple(total[i] for i in range(len(partials)))


def body(activations, out_grads, token_ids, forget_mask, importance, in_inverse, out_inverse):
    tok_rows, d_in = activations.shape
    total = tok_rows * lax.axis_size("fsdp")
    keep = 1.0 - forget_mask.astype(jnp.float32)
    weights = importance[token_ids] * keep / total
    forget_grads = out_grads * forget_mask.astype(jnp.bfloat16)[:, None]
    grad_scale = 1.0 / math.sqrt(total)

    gradient = scatter_sum(
        (transposed_term(activations, forget_grads) * grad_scale).astype(jnp.bfloat16)
    )

    def precondition(matrix):
        matrix_low = matrix.astype(jnp.bfloat16)
        mixed = add_columns(in_inverse, lax.all_gather(matrix_low, "fsdp", axis=0, tiled=True))
        mixed_low = mixed.astype(jnp.bfloat16)
        return jnp.dot(
            lax.all_gather(mixed_low, "fac", axis=1, tiled=True),
            out_inverse,
            preferred_element_type=jnp.float32,
        )

    def inner_part(left, right):
        return jnp.sum(left * right)

    residual = -gradient
    precond = precondition(residual)

    gram_cols = d_in // lax.axis_size("fac")
    own_cols = lax.dynamic_slice_in_dim(
        activations, lax.axis_index("fac") * gram_cols, gram_cols, axis=1
    )
    weighted = (own_cols * weights[:, None]).astype(jnp.bfloat16)
    gram_part = transposed_term(activations, weighted).astype(jnp.bfloat16)
    gram_rows = lax.all_gather(
        scatter_sum(gram_part).astype(jnp.bfloat16), "fac", axis=1, tiled=True
    )

    def curvature(matrix):
        matrix_low = matrix.astype(jnp.bfloat16)
        gathered = lax.all_gather(matrix_low, "fsdp", axis=0, tiled=True)
        return add_columns(gram_rows, gathered) + damping * matrix

    direction = precond
    image = curvature(direction)
    inner_now, energy = global_sums(inner_part(residual, precond), inner_part(direction, image))
    alpha = inner_now / energy
    newton_step = alpha * direction
    residual = residual - alpha * image

    precond = precondition(residual)
    precond_image = curvature(precond)
    inner_next, z_hz, z_hd, d_hz = global_sums(
        inner_part(residual, precond),
        inner_part(precond, precond_image),
        inner_part(precond, image),
        inner_part(direction, precond_image),
    )
    beta = inner_next / inner_now
    direction = precond + beta * direction
    image = precond_image + beta * image
    energy = z_hz + beta * (z_hd + d_hz) + beta * beta * energy
    alpha = inner_next / energy
    newton_step = newton_step + alpha * direction
    residual = residual - alpha * image
    return (newton_step, residual)


def solution(mesh):
    placed = (
        P("fsdp", None),
        P("fsdp", "fac"),
        P("fsdp"),
        P("fsdp"),
        P(),
        P("fsdp", None),
        P(None, "fac"),
    )
    return jax.shard_map(
        body,
        mesh=mesh,
        in_specs=placed,
        out_specs=(P("fsdp", "fac"), P("fsdp", "fac")),
        check_vma=False,
    )
```

```python
import math

import jax
import jax.numpy as jnp
from jax import lax
from jax.sharding import PartitionSpec as P

ITERS = 2


damping = 0.3


def add_columns(matrix, piece):
    return jnp.dot(matrix, piece, preferred_element_type=jnp.float32)


def transposed_term(matrix, right):
    return lax.dot_general(
        matrix, right, (((0,), (0,)), ((), ())), preferred_element_type=jnp.float32
    )


def scatter_sum(partial):
    parts = lax.axis_size("fsdp")
    blocks = partial.reshape(parts, partial.shape[0] // parts, partial.shape[1])
    received = lax.all_to_all(blocks, "fsdp", 0, 0, tiled=False)
    return jnp.sum(received.astype(jnp.float32), axis=0)


def global_sums(*partials):
    devices = lax.axis_size("fsdp") * lax.axis_size("fac")
    stacked = jnp.broadcast_to(jnp.stack(partials)[None, :], (devices, len(partials)))
    received = lax.all_to_all(stacked, ("fsdp", "fac"), 0, 0, tiled=True)
    total = jnp.sum(received, axis=0)
    return tuple(total[i] for i in range(len(partials)))


def body(activations, out_grads, token_ids, forget_mask, importance, in_inverse, out_inverse):
    tok_rows, d_in = activations.shape
    total = tok_rows * lax.axis_size("fsdp")
    keep = 1.0 - forget_mask.astype(jnp.float32)
    weights = importance[token_ids] * keep / total
    forget_grads = out_grads * forget_mask.astype(jnp.bfloat16)[:, None]
    grad_scale = 1.0 / math.sqrt(total)

    gradient = scatter_sum(
        (transposed_term(activations, forget_grads) * grad_scale).astype(jnp.bfloat16)
    )

    def gather_rows(matrix):
        return lax.all_gather(matrix.astype(jnp.bfloat16), "fsdp", axis=0, tiled=True)

    def precondition(gathered):
        mixed = add_columns(in_inverse, gathered)
        mixed_low = mixed.astype(jnp.bfloat16)
        return jnp.dot(
            lax.all_gather(mixed_low, "fac", axis=1, tiled=True),
            out_inverse,
            preferred_element_type=jnp.float32,
        )

    def inner_part(left, right):
        return jnp.sum(left * right)

    residual = -gradient
    residual_rows = gather_rows(residual)

    gram_cols = d_in // lax.axis_size("fac")
    own_cols = lax.dynamic_slice_in_dim(
        activations, lax.axis_index("fac") * gram_cols, gram_cols, axis=1
    )
    weighted = (own_cols * weights[:, None]).astype(jnp.bfloat16)
    gram_part = transposed_term(activations, weighted).astype(jnp.bfloat16)
    residual_rows, gram_part = lax.optimization_barrier((residual_rows, gram_part))
    precond = precondition(residual_rows)
    gram_rows = lax.all_gather(
        scatter_sum(gram_part).astype(jnp.bfloat16), "fac", axis=1, tiled=True
    )

    def curvature(matrix):
        return add_columns(gram_rows, gather_rows(matrix)) + damping * matrix

    direction = precond
    image = curvature(direction)
    image_rows = gather_rows(image)
    inner_now, energy = global_sums(inner_part(residual, precond), inner_part(direction, image))
    alpha = inner_now / energy
    newton_step = alpha * direction
    residual = residual - alpha * image
    next_rows = (
        residual_rows.astype(jnp.float32) - alpha * image_rows.astype(jnp.float32)
    ).astype(jnp.bfloat16)

    precond = precondition(next_rows)
    precond_image = curvature(precond)
    inner_next, z_hz, z_hd, d_hz = global_sums(
        inner_part(residual, precond),
        inner_part(precond, precond_image),
        inner_part(precond, image),
        inner_part(direction, precond_image),
    )
    beta = inner_next / inner_now
    direction = precond + beta * direction
    image = precond_image + beta * image
    energy = z_hz + beta * (z_hd + d_hz) + beta * beta * energy
    alpha = inner_next / energy
    newton_step = newton_step + alpha * direction
    residual = residual - alpha * image
    return (newton_step, residual)


def solution(mesh):
    placed = (
        P("fsdp", None),
        P("fsdp", "fac"),
        P("fsdp"),
        P("fsdp"),
        P(),
        P("fsdp", None),
        P(None, "fac"),
    )
    return jax.shard_map(
        body,
        mesh=mesh,
        in_specs=placed,
        out_specs=(P("fsdp", "fac"), P("fsdp", "fac")),
        check_vma=False,
    )
```

```python
import math

import jax
import jax.numpy as jnp
from jax import lax
from jax.sharding import PartitionSpec as P

ITERS = 2


damping = 0.3


def add_columns(matrix, piece):
    return jnp.dot(matrix, piece, preferred_element_type=jnp.float32)


def transposed_term(matrix, right):
    return lax.dot_general(
        matrix, right, (((0,), (0,)), ((), ())), preferred_element_type=jnp.float32
    )


def scatter_sum(partial):
    parts = lax.axis_size("fsdp")
    blocks = partial.reshape(parts, partial.shape[0] // parts, partial.shape[1])
    received = lax.all_to_all(blocks, "fsdp", 0, 0, tiled=False)
    return lax.optimization_barrier(jnp.sum(received.astype(jnp.float32), axis=0))


def global_sums(*partials):
    devices = lax.axis_size("fsdp") * lax.axis_size("fac")
    stacked = jnp.broadcast_to(jnp.stack(partials)[None, :], (devices, len(partials)))
    received = lax.all_to_all(stacked, ("fsdp", "fac"), 0, 0, tiled=True)
    total = jnp.sum(received, axis=0)
    return tuple(total[i] for i in range(len(partials)))


def body(activations, out_grads, token_ids, forget_mask, importance, in_inverse, out_inverse):
    tok_rows, d_in = activations.shape
    total = tok_rows * lax.axis_size("fsdp")
    keep = 1.0 - forget_mask.astype(jnp.float32)
    weights = importance[token_ids] * keep / total
    forget_grads = out_grads * forget_mask.astype(jnp.bfloat16)[:, None]
    grad_scale = 1.0 / math.sqrt(total)

    gradient = scatter_sum(
        (transposed_term(activations, forget_grads) * grad_scale).astype(jnp.bfloat16)
    )

    def gather_rows(matrix):
        return lax.all_gather(matrix.astype(jnp.bfloat16), "fsdp", axis=0, tiled=True)

    def precondition(gathered):
        mixed = add_columns(in_inverse, gathered)
        mixed_low = mixed.astype(jnp.bfloat16)
        return jnp.dot(
            lax.all_gather(mixed_low, "fac", axis=1, tiled=True),
            out_inverse,
            preferred_element_type=jnp.float32,
        )

    def inner_part(left, right):
        return jnp.sum(left * right)

    residual = -gradient
    residual_rows = gather_rows(residual)

    gram_cols = d_in // lax.axis_size("fac")
    own_cols = lax.dynamic_slice_in_dim(
        activations, lax.axis_index("fac") * gram_cols, gram_cols, axis=1
    )
    weighted = (own_cols * weights[:, None]).astype(jnp.bfloat16)
    half = gram_cols // 2
    gram_first = transposed_term(activations, weighted[:, :half]).astype(jnp.bfloat16)
    gram_second = transposed_term(activations, weighted[:, half:]).astype(jnp.bfloat16)
    residual_rows, first_rows = lax.optimization_barrier((residual_rows, scatter_sum(gram_first)))
    precond = precondition(residual_rows)
    gram_own = jnp.concatenate([first_rows, scatter_sum(gram_second)], axis=1)
    gram_rows = lax.all_gather(gram_own.astype(jnp.bfloat16), "fac", axis=1, tiled=True)

    def curvature(matrix):
        return add_columns(gram_rows, gather_rows(matrix)) + damping * matrix

    direction = precond
    image = curvature(direction)
    image_rows = gather_rows(image)
    inner_now, energy = global_sums(inner_part(residual, precond), inner_part(direction, image))
    alpha = inner_now / energy
    newton_step = alpha * direction
    residual = residual - alpha * image
    next_rows = (
        residual_rows.astype(jnp.float32) - alpha * image_rows.astype(jnp.float32)
    ).astype(jnp.bfloat16)

    precond = precondition(next_rows)
    precond_image = curvature(precond)
    inner_next, z_hz, z_hd, d_hz = global_sums(
        inner_part(residual, precond),
        inner_part(precond, precond_image),
        inner_part(precond, image),
        inner_part(direction, precond_image),
    )
    beta = inner_next / inner_now
    direction = precond + beta * direction
    image = precond_image + beta * image
    energy = z_hz + beta * (z_hd + d_hz) + beta * beta * energy
    alpha = inner_next / energy
    newton_step = newton_step + alpha * direction
    residual = residual - alpha * image
    return (newton_step, residual)


def solution(mesh):
    placed = (
        P("fsdp", None),
        P("fsdp", "fac"),
        P("fsdp"),
        P("fsdp"),
        P(),
        P("fsdp", None),
        P(None, "fac"),
    )
    return jax.shard_map(
        body,
        mesh=mesh,
        in_specs=placed,
        out_specs=(P("fsdp", "fac"), P("fsdp", "fac")),
        check_vma=False,
    )
```

```python
import math

import jax
import jax.numpy as jnp
from jax import lax
from jax.sharding import PartitionSpec as P

ITERS = 2


damping = 0.3


def add_columns(matrix, piece):
    return jnp.dot(matrix, piece, preferred_element_type=jnp.float32)


def transposed_term(matrix, right):
    return lax.dot_general(
        matrix, right, (((0,), (0,)), ((), ())), preferred_element_type=jnp.float32
    )


FSDP = ("pairs", "core")


def scatter_sum(partial):
    pairs, cores = lax.axis_size("pairs"), lax.axis_size("core")
    blocks = partial.reshape(pairs, cores, partial.shape[0] // (pairs * cores), partial.shape[1])
    on_chip = lax.all_to_all(blocks, "core", 1, 1, tiled=False)
    chip_sum = jnp.sum(on_chip.astype(jnp.float32), axis=1).astype(jnp.bfloat16)
    received = lax.all_to_all(chip_sum, "pairs", 0, 0, tiled=False)
    return lax.optimization_barrier(jnp.sum(received.astype(jnp.float32), axis=0))


def global_sums(*partials):
    devices = lax.axis_size("pairs") * lax.axis_size("core") * lax.axis_size("fac")
    stacked = jnp.broadcast_to(jnp.stack(partials)[None, :], (devices, len(partials)))
    received = lax.all_to_all(stacked, FSDP + ("fac",), 0, 0, tiled=True)
    total = jnp.sum(received, axis=0)
    return tuple(total[i] for i in range(len(partials)))


def body(activations, out_grads, token_ids, forget_mask, importance, in_inverse, out_inverse):
    tok_rows, d_in = activations.shape
    total = tok_rows * lax.axis_size("pairs") * lax.axis_size("core")
    keep = 1.0 - forget_mask.astype(jnp.float32)
    weights = importance[token_ids] * keep / total
    forget_grads = out_grads * forget_mask.astype(jnp.bfloat16)[:, None]
    grad_scale = 1.0 / math.sqrt(total)

    gradient = scatter_sum(
        (transposed_term(activations, forget_grads) * grad_scale).astype(jnp.bfloat16)
    )

    def gather_rows(matrix):
        return lax.all_gather(matrix.astype(jnp.bfloat16), FSDP, axis=0, tiled=True)

    def precondition(gathered):
        mixed = add_columns(in_inverse, gathered)
        mixed_low = mixed.astype(jnp.bfloat16)
        return jnp.dot(
            lax.all_gather(mixed_low, "fac", axis=1, tiled=True),
            out_inverse,
            preferred_element_type=jnp.float32,
        )

    def inner_part(left, right):
        return jnp.sum(left * right)

    residual = -gradient
    residual_rows = gather_rows(residual)

    gram_cols = d_in // lax.axis_size("fac")
    own_cols = lax.dynamic_slice_in_dim(
        activations, lax.axis_index("fac") * gram_cols, gram_cols, axis=1
    )
    weighted = (own_cols * weights[:, None]).astype(jnp.bfloat16)
    half = gram_cols // 2
    gram_first = transposed_term(activations, weighted[:, :half]).astype(jnp.bfloat16)
    gram_second = transposed_term(activations, weighted[:, half:]).astype(jnp.bfloat16)
    residual_rows, first_rows = lax.optimization_barrier((residual_rows, scatter_sum(gram_first)))
    precond = precondition(residual_rows)
    gram_own = jnp.concatenate([first_rows, scatter_sum(gram_second)], axis=1)
    gram_rows = lax.all_gather(gram_own.astype(jnp.bfloat16), "fac", axis=1, tiled=True)

    def curvature(matrix):
        return add_columns(gram_rows, gather_rows(matrix)) + damping * matrix

    direction = precond
    image = curvature(direction)
    image_rows = gather_rows(image)
    inner_now, energy = global_sums(inner_part(residual, precond), inner_part(direction, image))
    alpha = inner_now / energy
    newton_step = alpha * direction
    residual = residual - alpha * image
    next_rows = (
        residual_rows.astype(jnp.float32) - alpha * image_rows.astype(jnp.float32)
    ).astype(jnp.bfloat16)

    precond = precondition(next_rows)
    precond_image = curvature(precond)
    inner_next, z_hz, z_hd, d_hz = global_sums(
        inner_part(residual, precond),
        inner_part(precond, precond_image),
        inner_part(precond, image),
        inner_part(direction, precond_image),
    )
    beta = inner_next / inner_now
    direction = precond + beta * direction
    image = precond_image + beta * image
    energy = z_hz + beta * (z_hd + d_hz) + beta * beta * energy
    alpha = inner_next / energy
    newton_step = newton_step + alpha * direction
    residual = residual - alpha * image
    return (newton_step, residual)


def solution(mesh):
    cores = 2
    split = jax.sharding.Mesh(
        mesh.devices.reshape(mesh.shape["fsdp"] // cores, cores, mesh.shape["fac"]),
        ("pairs", "core", "fac"),
    )
    placed = (
        P(FSDP, None),
        P(FSDP, "fac"),
        P(FSDP),
        P(FSDP),
        P(),
        P(FSDP, None),
        P(None, "fac"),
    )
    return jax.shard_map(
        body,
        mesh=split,
        in_specs=placed,
        out_specs=(P(FSDP, "fac"), P(FSDP, "fac")),
        check_vma=False,
    )
```

```python
import math

import jax
import jax.numpy as jnp
from jax import lax
from jax.sharding import PartitionSpec as P

ITERS = 2


damping = 0.3


def add_columns(matrix, piece):
    return jnp.dot(matrix, piece, preferred_element_type=jnp.float32)


def transposed_term(matrix, right):
    return lax.dot_general(
        matrix, right, (((0,), (0,)), ((), ())), preferred_element_type=jnp.float32
    )


FSDP = ("pairs", "core")


def stacked_product(pieces, right):
    return lax.dot_general(
        pieces,
        right.reshape(pieces.shape[0], pieces.shape[2], right.shape[1]),
        (((0, 2), (0, 1)), ((), ())),
        preferred_element_type=jnp.float32,
    )


def scatter_sum(partial):
    pairs, cores = lax.axis_size("pairs"), lax.axis_size("core")
    blocks = partial.reshape(pairs, cores, partial.shape[0] // (pairs * cores), partial.shape[1])
    on_chip = lax.all_to_all(blocks, "core", 1, 1, tiled=False)
    chip_sum = jnp.sum(on_chip.astype(jnp.float32), axis=1).astype(jnp.bfloat16)
    received = lax.all_to_all(chip_sum, "pairs", 0, 0, tiled=False)
    return lax.optimization_barrier(jnp.sum(received.astype(jnp.float32), axis=0))


def global_sums(*partials):
    devices = lax.axis_size("pairs") * lax.axis_size("core") * lax.axis_size("fac")
    stacked = jnp.broadcast_to(jnp.stack(partials)[None, :], (devices, len(partials)))
    received = lax.all_to_all(stacked, FSDP + ("fac",), 0, 0, tiled=True)
    total = jnp.sum(received, axis=0)
    return tuple(total[i] for i in range(len(partials)))


def body(activations, out_grads, token_ids, forget_mask, importance, in_inverse, out_inverse):
    tok_rows, d_in = activations.shape
    total = tok_rows * lax.axis_size("pairs") * lax.axis_size("core")
    keep = 1.0 - forget_mask.astype(jnp.float32)
    weights = importance[token_ids] * keep / total
    forget_grads = out_grads * forget_mask.astype(jnp.bfloat16)[:, None]
    grad_scale = 1.0 / math.sqrt(total)

    gradient = scatter_sum(
        (transposed_term(activations, forget_grads) * grad_scale).astype(jnp.bfloat16)
    )

    def gather_rows(matrix):
        return lax.all_gather(matrix.astype(jnp.bfloat16), FSDP, axis=0, tiled=True)

    def precondition(gathered):
        mixed = add_columns(in_inverse, gathered)
        mixed_low = mixed.astype(jnp.bfloat16)
        return stacked_product(lax.all_gather(mixed_low, "fac", axis=0), out_inverse)

    def inner_part(left, right):
        return jnp.sum(left * right)

    residual = -gradient
    residual_rows = gather_rows(residual)

    gram_cols = d_in // lax.axis_size("fac")
    own_cols = lax.dynamic_slice_in_dim(
        activations, lax.axis_index("fac") * gram_cols, gram_cols, axis=1
    )
    weighted = (own_cols * weights[:, None]).astype(jnp.bfloat16)
    half = gram_cols // 2
    gram_first = transposed_term(activations, weighted[:, :half]).astype(jnp.bfloat16)
    gram_second = transposed_term(activations, weighted[:, half:]).astype(jnp.bfloat16)
    residual_rows, first_rows = lax.optimization_barrier((residual_rows, scatter_sum(gram_first)))
    precond = precondition(residual_rows)
    gram_own = jnp.concatenate([first_rows, scatter_sum(gram_second)], axis=1)
    gram_rows = lax.all_gather(gram_own.astype(jnp.bfloat16), "fac", axis=0)

    def curvature(matrix):
        return stacked_product(gram_rows, gather_rows(matrix)) + damping * matrix

    direction = precond
    image = curvature(direction)
    image_rows = gather_rows(image)
    inner_now, energy = global_sums(inner_part(residual, precond), inner_part(direction, image))
    alpha = inner_now / energy
    newton_step = alpha * direction
    residual = residual - alpha * image
    next_rows = (
        residual_rows.astype(jnp.float32) - alpha * image_rows.astype(jnp.float32)
    ).astype(jnp.bfloat16)

    precond = precondition(next_rows)
    precond_image = curvature(precond)
    inner_next, z_hz, z_hd, d_hz = global_sums(
        inner_part(residual, precond),
        inner_part(precond, precond_image),
        inner_part(precond, image),
        inner_part(direction, precond_image),
    )
    beta = inner_next / inner_now
    direction = precond + beta * direction
    image = precond_image + beta * image
    energy = z_hz + beta * (z_hd + d_hz) + beta * beta * energy
    alpha = inner_next / energy
    newton_step = newton_step + alpha * direction
    residual = residual - alpha * image
    return (newton_step, residual)


def solution(mesh):
    cores = 2
    split = jax.sharding.Mesh(
        mesh.devices.reshape(mesh.shape["fsdp"] // cores, cores, mesh.shape["fac"]),
        ("pairs", "core", "fac"),
    )
    placed = (
        P(FSDP, None),
        P(FSDP, "fac"),
        P(FSDP),
        P(FSDP),
        P(),
        P(FSDP, None),
        P(None, "fac"),
    )
    return jax.shard_map(
        body,
        mesh=split,
        in_specs=placed,
        out_specs=(P(FSDP, "fac"), P(FSDP, "fac")),
        check_vma=False,
    )
```

```python
import math

import jax
import jax.numpy as jnp
from jax import lax
from jax.sharding import PartitionSpec as P

ITERS = 2


damping = 0.3


def add_columns(matrix, piece):
    return jnp.dot(matrix, piece, preferred_element_type=jnp.float32)


def transposed_term(matrix, right):
    return lax.dot_general(
        matrix, right, (((0,), (0,)), ((), ())), preferred_element_type=jnp.float32
    )


FSDP = ("pairs", "core")


def scatter_sum(partial):
    pairs, cores = lax.axis_size("pairs"), lax.axis_size("core")
    blocks = partial.reshape(pairs, cores, partial.shape[0] // (pairs * cores), partial.shape[1])
    on_chip = lax.all_to_all(blocks, "core", 1, 1, tiled=False)
    chip_sum = jnp.sum(on_chip.astype(jnp.float32), axis=1).astype(jnp.bfloat16)
    received = lax.all_to_all(chip_sum, "pairs", 0, 0, tiled=False)
    return lax.optimization_barrier(jnp.sum(received.astype(jnp.float32), axis=0))


def global_sums(*partials):
    devices = lax.axis_size("pairs") * lax.axis_size("core") * lax.axis_size("fac")
    stacked = jnp.broadcast_to(jnp.stack(partials)[None, :], (devices, len(partials)))
    received = lax.all_to_all(stacked, FSDP + ("fac",), 0, 0, tiled=True)
    total = jnp.sum(received, axis=0)
    return tuple(total[i] for i in range(len(partials)))


def body(activations, out_grads, token_ids, forget_mask, importance, in_inverse, out_inverse):
    tok_rows, d_in = activations.shape
    total = tok_rows * lax.axis_size("pairs") * lax.axis_size("core")
    keep = 1.0 - forget_mask.astype(jnp.float32)
    weights = importance[token_ids] * keep / total
    forget_grads = out_grads * forget_mask.astype(jnp.bfloat16)[:, None]
    grad_scale = 1.0 / math.sqrt(total)

    gradient = scatter_sum(
        (transposed_term(activations, forget_grads) * grad_scale).astype(jnp.bfloat16)
    )

    def gather_rows(matrix):
        return lax.all_gather(matrix.astype(jnp.bfloat16), FSDP, axis=0, tiled=True)

    def precondition(gathered):
        mixed = add_columns(in_inverse, gathered)
        mixed_low = mixed.astype(jnp.bfloat16)
        return jnp.dot(
            lax.all_gather(mixed_low, "fac", axis=1, tiled=True),
            out_inverse,
            preferred_element_type=jnp.float32,
        )

    def inner_part(left, right):
        return jnp.sum(left * right)

    d_out_part = out_inverse.shape[1]
    in_cols = lax.all_gather(
        lax.dynamic_slice_in_dim(in_inverse, lax.axis_index("fac") * d_out_part, d_out_part, axis=1),
        FSDP,
        axis=0,
        tiled=True,
    )

    gradient, in_cols = lax.optimization_barrier((gradient, in_cols))
    residual = -gradient
    residual_rows = gather_rows(residual)

    gram_cols = d_in // lax.axis_size("fac")
    own_cols = lax.dynamic_slice_in_dim(
        activations, lax.axis_index("fac") * gram_cols, gram_cols, axis=1
    )
    weighted = (own_cols * weights[:, None]).astype(jnp.bfloat16)
    half = gram_cols // 2
    gram_first = transposed_term(activations, weighted[:, :half]).astype(jnp.bfloat16)
    gram_second = transposed_term(activations, weighted[:, half:]).astype(jnp.bfloat16)
    residual_rows, first_rows = lax.optimization_barrier((residual_rows, scatter_sum(gram_first)))
    precond = precondition(residual_rows)
    gram_own = jnp.concatenate([first_rows, scatter_sum(gram_second)], axis=1)
    gram_rows = lax.all_gather(gram_own.astype(jnp.bfloat16), "fac", axis=1, tiled=True)

    def curvature(matrix):
        return add_columns(gram_rows, gather_rows(matrix)) + damping * matrix

    direction = precond
    image = curvature(direction)
    image_rows = gather_rows(image)
    inner_now, energy = global_sums(inner_part(residual, precond), inner_part(direction, image))
    gram_inverse = lax.all_gather(
        add_columns(gram_rows, in_cols).astype(jnp.bfloat16), "fac", axis=1, tiled=True
    )
    alpha = inner_now / energy
    newton_step = alpha * direction
    residual = residual - alpha * image
    next_rows = (
        residual_rows.astype(jnp.float32) - alpha * image_rows.astype(jnp.float32)
    ).astype(jnp.bfloat16)

    rows = in_inverse.shape[0]
    left = jnp.concatenate([in_inverse, gram_inverse], axis=0)
    both = add_columns(left, next_rows).astype(jnp.bfloat16)
    both_out = jnp.dot(
        lax.all_gather(both, "fac", axis=1, tiled=True), out_inverse, preferred_element_type=jnp.float32
    )
    precond = both_out[:rows]
    precond_image = both_out[rows:] + damping * precond
    inner_next, z_hz, z_hd, d_hz = global_sums(
        inner_part(residual, precond),
        inner_part(precond, precond_image),
        inner_part(precond, image),
        inner_part(direction, precond_image),
    )
    beta = inner_next / inner_now
    direction = precond + beta * direction
    image = precond_image + beta * image
    energy = z_hz + beta * (z_hd + d_hz) + beta * beta * energy
    alpha = inner_next / energy
    newton_step = newton_step + alpha * direction
    residual = residual - alpha * image
    return (newton_step, residual)


def solution(mesh):
    cores = 2
    split = jax.sharding.Mesh(
        mesh.devices.reshape(mesh.shape["fsdp"] // cores, cores, mesh.shape["fac"]),
        ("pairs", "core", "fac"),
    )
    placed = (
        P(FSDP, None),
        P(FSDP, "fac"),
        P(FSDP),
        P(FSDP),
        P(),
        P(FSDP, None),
        P(None, "fac"),
    )
    return jax.shard_map(
        body,
        mesh=split,
        in_specs=placed,
        out_specs=(P(FSDP, "fac"), P(FSDP, "fac")),
        check_vma=False,
    )
```

```python
import math

import jax
import jax.numpy as jnp
from jax import lax
from jax.sharding import PartitionSpec as P

ITERS = 2


damping = 0.3


def add_columns(matrix, piece):
    return jnp.dot(matrix, piece, preferred_element_type=jnp.float32)


def transposed_term(matrix, right):
    return lax.dot_general(
        matrix, right, (((0,), (0,)), ((), ())), preferred_element_type=jnp.float32
    )


FSDP = ("pairs", "core")


def ring_product(piece, right):
    n = lax.axis_size("fac")
    me = lax.axis_index("fac")
    width = piece.shape[1]

    def right_block(k):
        return lax.dynamic_slice_in_dim(right, (k % n) * width, width, axis=0)

    total = add_columns(piece, right_block(me))
    ahead = piece
    behind = piece
    for step in range(1, n // 2 + 1):
        ahead = lax.ppermute(ahead, "fac", [(j, (j + 1) % n) for j in range(n)])
        total = total + add_columns(ahead, right_block(me - step))
        if 2 * step < n:
            behind = lax.ppermute(behind, "fac", [(j, (j - 1) % n) for j in range(n)])
            total = total + add_columns(behind, right_block(me + step))
    return total


def scatter_sum(partial):
    pairs, cores = lax.axis_size("pairs"), lax.axis_size("core")
    blocks = partial.reshape(pairs, cores, partial.shape[0] // (pairs * cores), partial.shape[1])
    on_chip = lax.all_to_all(blocks, "core", 1, 1, tiled=False)
    chip_sum = jnp.sum(on_chip.astype(jnp.float32), axis=1).astype(jnp.bfloat16)
    received = lax.all_to_all(chip_sum, "pairs", 0, 0, tiled=False)
    return lax.optimization_barrier(jnp.sum(received.astype(jnp.float32), axis=0))


def global_sums(*partials):
    devices = lax.axis_size("pairs") * lax.axis_size("core") * lax.axis_size("fac")
    stacked = jnp.broadcast_to(jnp.stack(partials)[None, :], (devices, len(partials)))
    received = lax.all_to_all(stacked, FSDP + ("fac",), 0, 0, tiled=True)
    total = jnp.sum(received, axis=0)
    return tuple(total[i] for i in range(len(partials)))


def body(activations, out_grads, token_ids, forget_mask, importance, in_inverse, out_inverse):
    tok_rows, d_in = activations.shape
    total = tok_rows * lax.axis_size("pairs") * lax.axis_size("core")
    keep = 1.0 - forget_mask.astype(jnp.float32)
    weights = importance[token_ids] * keep / total
    forget_grads = out_grads * forget_mask.astype(jnp.bfloat16)[:, None]
    grad_scale = 1.0 / math.sqrt(total)

    gradient = scatter_sum(
        (transposed_term(activations, forget_grads) * grad_scale).astype(jnp.bfloat16)
    )

    def gather_rows(matrix):
        return lax.all_gather(matrix.astype(jnp.bfloat16), FSDP, axis=0, tiled=True)

    def precondition(gathered):
        mixed = add_columns(in_inverse, gathered)
        mixed_low = mixed.astype(jnp.bfloat16)
        return jnp.dot(
            lax.all_gather(mixed_low, "fac", axis=1, tiled=True),
            out_inverse,
            preferred_element_type=jnp.float32,
        )

    def inner_part(left, right):
        return jnp.sum(left * right)

    d_out_part = out_inverse.shape[1]
    in_cols = lax.all_gather(
        lax.dynamic_slice_in_dim(in_inverse, lax.axis_index("fac") * d_out_part, d_out_part, axis=1),
        FSDP,
        axis=0,
        tiled=True,
    )

    gradient, in_cols = lax.optimization_barrier((gradient, in_cols))
    residual = -gradient
    residual_rows = gather_rows(residual)

    gram_cols = d_in // lax.axis_size("fac")
    own_cols = lax.dynamic_slice_in_dim(
        activations, lax.axis_index("fac") * gram_cols, gram_cols, axis=1
    )
    weighted = (own_cols * weights[:, None]).astype(jnp.bfloat16)
    half = gram_cols // 2
    gram_first = transposed_term(activations, weighted[:, :half]).astype(jnp.bfloat16)
    gram_second = transposed_term(activations, weighted[:, half:]).astype(jnp.bfloat16)
    residual_rows, first_rows = lax.optimization_barrier((residual_rows, scatter_sum(gram_first)))
    precond = precondition(residual_rows)
    gram_own = jnp.concatenate([first_rows, scatter_sum(gram_second)], axis=1)
    gram_rows = lax.all_gather(gram_own.astype(jnp.bfloat16), "fac", axis=1, tiled=True)

    def curvature(matrix):
        return add_columns(gram_rows, gather_rows(matrix)) + damping * matrix

    direction = precond
    image = curvature(direction)
    image_rows = gather_rows(image)
    inner_now, energy = global_sums(inner_part(residual, precond), inner_part(direction, image))
    gram_inverse = lax.all_gather(
        add_columns(gram_rows, in_cols).astype(jnp.bfloat16), "fac", axis=1, tiled=True
    )
    alpha = inner_now / energy
    newton_step = alpha * direction
    residual = residual - alpha * image
    next_rows = (
        residual_rows.astype(jnp.float32) - alpha * image_rows.astype(jnp.float32)
    ).astype(jnp.bfloat16)

    rows = in_inverse.shape[0]
    left = jnp.concatenate([in_inverse, gram_inverse], axis=0)
    both = add_columns(left, next_rows).astype(jnp.bfloat16)
    both_out = ring_product(both, out_inverse)
    precond = both_out[:rows]
    precond_image = both_out[rows:] + damping * precond
    inner_next, z_hz, z_hd, d_hz = global_sums(
        inner_part(residual, precond),
        inner_part(precond, precond_image),
        inner_part(precond, image),
        inner_part(direction, precond_image),
    )
    beta = inner_next / inner_now
    direction = precond + beta * direction
    image = precond_image + beta * image
    energy = z_hz + beta * (z_hd + d_hz) + beta * beta * energy
    alpha = inner_next / energy
    newton_step = newton_step + alpha * direction
    residual = residual - alpha * image
    return (newton_step, residual)


def solution(mesh):
    cores = 2
    split = jax.sharding.Mesh(
        mesh.devices.reshape(mesh.shape["fsdp"] // cores, cores, mesh.shape["fac"]),
        ("pairs", "core", "fac"),
    )
    placed = (
        P(FSDP, None),
        P(FSDP, "fac"),
        P(FSDP),
        P(FSDP),
        P(),
        P(FSDP, None),
        P(None, "fac"),
    )
    return jax.shard_map(
        body,
        mesh=split,
        in_specs=placed,
        out_specs=(P(FSDP, "fac"), P(FSDP, "fac")),
        check_vma=False,
    )
```

```python
import math

import jax
import jax.numpy as jnp
from jax import lax
from jax.experimental import pallas as pl
from jax.sharding import PartitionSpec as P

ITERS = 2


damping = 0.3


def add_columns(matrix, piece):
    return jnp.dot(matrix, piece, preferred_element_type=jnp.float32)


def transposed_term(matrix, right):
    return lax.dot_general(
        matrix, right, (((0,), (0,)), ((), ())), preferred_element_type=jnp.float32
    )


FSDP = ("pairs", "core")


def ring_product(piece, right):
    n = lax.axis_size("fac")
    me = lax.axis_index("fac")
    width = piece.shape[1]

    def right_block(k):
        return lax.dynamic_slice_in_dim(right, (k % n) * width, width, axis=0)

    total = add_columns(piece, right_block(me))
    ahead = piece
    behind = piece
    for step in range(1, n // 2 + 1):
        ahead = lax.ppermute(ahead, "fac", [(j, (j + 1) % n) for j in range(n)])
        total = total + add_columns(ahead, right_block(me - step))
        if 2 * step < n:
            behind = lax.ppermute(behind, "fac", [(j, (j - 1) % n) for j in range(n)])
            total = total + add_columns(behind, right_block(me + step))
    return total


def block_term(acts_t, right, scale):
    pairs, cores = lax.axis_size("pairs"), lax.axis_size("core")
    rows = acts_t.shape[0] // (pairs * cores)
    tokens, cols = right.shape

    def kernel(a_ref, x_ref, o_ref):
        product = jnp.dot(a_ref[...], x_ref[...], preferred_element_type=jnp.float32)
        o_ref[0, 0] = (product * scale).astype(o_ref.dtype)

    return pl.pallas_call(
        kernel,
        grid=(cores, pairs),
        in_specs=[
            pl.BlockSpec((rows, tokens), lambda k, p: (p * cores + k, 0)),
            pl.BlockSpec((tokens, cols), lambda k, p: (0, 0)),
        ],
        out_specs=pl.BlockSpec((1, 1, rows, cols), lambda k, p: (k, p, 0, 0)),
        out_shape=jax.ShapeDtypeStruct((cores, pairs, rows, cols), jnp.bfloat16),
    )(acts_t, right)


def scatter_sum(blocks):
    on_chip = lax.all_to_all(blocks, "core", 0, 0, tiled=False)
    chip_sum = jnp.sum(on_chip.astype(jnp.float32), axis=0).astype(jnp.bfloat16)
    received = lax.all_to_all(chip_sum, "pairs", 0, 0, tiled=False)
    return lax.optimization_barrier(jnp.sum(received.astype(jnp.float32), axis=0))


def global_sums(*partials):
    devices = lax.axis_size("pairs") * lax.axis_size("core") * lax.axis_size("fac")
    stacked = jnp.broadcast_to(jnp.stack(partials)[None, :], (devices, len(partials)))
    received = lax.all_to_all(stacked, FSDP + ("fac",), 0, 0, tiled=True)
    total = jnp.sum(received, axis=0)
    return tuple(total[i] for i in range(len(partials)))


def body(activations, out_grads, token_ids, forget_mask, importance, in_inverse, out_inverse):
    tok_rows, d_in = activations.shape
    total = tok_rows * lax.axis_size("pairs") * lax.axis_size("core")
    keep = 1.0 - forget_mask.astype(jnp.float32)
    weights = importance[token_ids] * keep / total
    forget_grads = out_grads * forget_mask.astype(jnp.bfloat16)[:, None]
    grad_scale = 1.0 / math.sqrt(total)

    acts_t = activations.T
    gradient = scatter_sum(block_term(acts_t, forget_grads, grad_scale))

    def gather_rows(matrix):
        return lax.all_gather(matrix.astype(jnp.bfloat16), FSDP, axis=0, tiled=True)

    def precondition(gathered):
        mixed = add_columns(in_inverse, gathered)
        mixed_low = mixed.astype(jnp.bfloat16)
        return jnp.dot(
            lax.all_gather(mixed_low, "fac", axis=1, tiled=True),
            out_inverse,
            preferred_element_type=jnp.float32,
        )

    def inner_part(left, right):
        return jnp.sum(left * right)

    d_out_part = out_inverse.shape[1]
    in_cols = lax.all_gather(
        lax.dynamic_slice_in_dim(in_inverse, lax.axis_index("fac") * d_out_part, d_out_part, axis=1),
        FSDP,
        axis=0,
        tiled=True,
    )

    gradient, in_cols = lax.optimization_barrier((gradient, in_cols))
    residual = -gradient
    residual_rows = gather_rows(residual)

    gram_cols = d_in // lax.axis_size("fac")
    own_cols = lax.dynamic_slice_in_dim(
        activations, lax.axis_index("fac") * gram_cols, gram_cols, axis=1
    )
    weighted = (own_cols * weights[:, None]).astype(jnp.bfloat16)
    half = gram_cols // 2
    gram_first = block_term(acts_t, weighted[:, :half], 1.0)
    gram_second = block_term(acts_t, weighted[:, half:], 1.0)
    residual_rows, first_rows = lax.optimization_barrier((residual_rows, scatter_sum(gram_first)))
    precond = precondition(residual_rows)
    gram_own = jnp.concatenate([first_rows, scatter_sum(gram_second)], axis=1)
    gram_rows = lax.all_gather(gram_own.astype(jnp.bfloat16), "fac", axis=1, tiled=True)

    def curvature(matrix):
        return add_columns(gram_rows, gather_rows(matrix)) + damping * matrix

    direction = precond
    image = curvature(direction)
    image_rows = gather_rows(image)
    inner_now, energy = global_sums(inner_part(residual, precond), inner_part(direction, image))
    gram_inverse = lax.all_gather(
        add_columns(gram_rows, in_cols).astype(jnp.bfloat16), "fac", axis=1, tiled=True
    )
    alpha = inner_now / energy
    newton_step = alpha * direction
    residual = residual - alpha * image
    next_rows = (
        residual_rows.astype(jnp.float32) - alpha * image_rows.astype(jnp.float32)
    ).astype(jnp.bfloat16)

    rows = in_inverse.shape[0]
    left = jnp.concatenate([in_inverse, gram_inverse], axis=0)
    both = add_columns(left, next_rows).astype(jnp.bfloat16)
    both_out = ring_product(both, out_inverse)
    precond = both_out[:rows]
    precond_image = both_out[rows:] + damping * precond
    inner_next, z_hz, z_hd, d_hz = global_sums(
        inner_part(residual, precond),
        inner_part(precond, precond_image),
        inner_part(precond, image),
        inner_part(direction, precond_image),
    )
    beta = inner_next / inner_now
    direction = precond + beta * direction
    image = precond_image + beta * image
    energy = z_hz + beta * (z_hd + d_hz) + beta * beta * energy
    alpha = inner_next / energy
    newton_step = newton_step + alpha * direction
    residual = residual - alpha * image
    return (newton_step, residual)


def solution(mesh):
    cores = 2
    split = jax.sharding.Mesh(
        mesh.devices.reshape(mesh.shape["fsdp"] // cores, cores, mesh.shape["fac"]),
        ("pairs", "core", "fac"),
    )
    placed = (
        P(FSDP, None),
        P(FSDP, "fac"),
        P(FSDP),
        P(FSDP),
        P(),
        P(FSDP, None),
        P(None, "fac"),
    )
    return jax.shard_map(
        body,
        mesh=split,
        in_specs=placed,
        out_specs=(P(FSDP, "fac"), P(FSDP, "fac")),
        check_vma=False,
    )
```

```python
import math

import jax
import jax.numpy as jnp
from jax import lax
from jax.experimental import pallas as pl
from jax.sharding import PartitionSpec as P

ITERS = 2


damping = 0.3


def add_columns(matrix, piece):
    return jnp.dot(matrix, piece, preferred_element_type=jnp.float32)


def transposed_term(matrix, right):
    return lax.dot_general(
        matrix, right, (((0,), (0,)), ((), ())), preferred_element_type=jnp.float32
    )


FSDP = ("pairs", "core")


def ring_product(piece, right):
    n = lax.axis_size("fac")
    me = lax.axis_index("fac")
    width = piece.shape[1]

    def right_block(k):
        return lax.dynamic_slice_in_dim(right, (k % n) * width, width, axis=0)

    total = add_columns(piece, right_block(me))
    ahead = piece
    behind = piece
    for step in range(1, n // 2 + 1):
        ahead = lax.ppermute(ahead, "fac", [(j, (j + 1) % n) for j in range(n)])
        total = total + add_columns(ahead, right_block(me - step))
        if 2 * step < n:
            behind = lax.ppermute(behind, "fac", [(j, (j - 1) % n) for j in range(n)])
            total = total + add_columns(behind, right_block(me + step))
    return total


def block_term(activations, right, scale):
    pairs, cores = lax.axis_size("pairs"), lax.axis_size("core")
    tokens, d_in = activations.shape
    rows = d_in // (pairs * cores)
    cols = right.shape[1]
    step = 384 if cols % 384 == 0 else cols

    def kernel(a_ref, x_ref, o_ref):
        product = lax.dot_general(
            a_ref[...], x_ref[...], (((0,), (0,)), ((), ())), preferred_element_type=jnp.float32
        )
        product = (product * scale).astype(o_ref.dtype)
        for block in range(pairs * cores):
            o_ref[block % cores, block // cores] = product[block * rows : (block + 1) * rows]

    return pl.pallas_call(
        kernel,
        grid=(cols // step,),
        in_specs=[
            pl.BlockSpec((tokens, d_in), lambda j: (0, 0)),
            pl.BlockSpec((tokens, step), lambda j: (0, j)),
        ],
        out_specs=pl.BlockSpec((cores, pairs, rows, step), lambda j: (0, 0, 0, j)),
        out_shape=jax.ShapeDtypeStruct((cores, pairs, rows, cols), jnp.bfloat16),
    )(activations, right)


def scatter_sum(blocks):
    on_chip = lax.all_to_all(blocks, "core", 0, 0, tiled=False)
    chip_sum = jnp.sum(on_chip.astype(jnp.float32), axis=0).astype(jnp.bfloat16)
    received = lax.all_to_all(chip_sum, "pairs", 0, 0, tiled=False)
    return lax.optimization_barrier(jnp.sum(received.astype(jnp.float32), axis=0))


def global_sums(*partials):
    devices = lax.axis_size("pairs") * lax.axis_size("core") * lax.axis_size("fac")
    stacked = jnp.broadcast_to(jnp.stack(partials)[None, :], (devices, len(partials)))
    received = lax.all_to_all(stacked, FSDP + ("fac",), 0, 0, tiled=True)
    total = jnp.sum(received, axis=0)
    return tuple(total[i] for i in range(len(partials)))


def body(activations, out_grads, token_ids, forget_mask, importance, in_inverse, out_inverse):
    tok_rows, d_in = activations.shape
    total = tok_rows * lax.axis_size("pairs") * lax.axis_size("core")
    keep = 1.0 - forget_mask.astype(jnp.float32)
    weights = importance[token_ids] * keep / total
    forget_grads = out_grads * forget_mask.astype(jnp.bfloat16)[:, None]
    grad_scale = 1.0 / math.sqrt(total)

    gradient = scatter_sum(block_term(activations, forget_grads, grad_scale))

    def gather_rows(matrix):
        return lax.all_gather(matrix.astype(jnp.bfloat16), FSDP, axis=0, tiled=True)

    def precondition(gathered):
        mixed = add_columns(in_inverse, gathered)
        mixed_low = mixed.astype(jnp.bfloat16)
        return jnp.dot(
            lax.all_gather(mixed_low, "fac", axis=1, tiled=True),
            out_inverse,
            preferred_element_type=jnp.float32,
        )

    def inner_part(left, right):
        return jnp.sum(left * right)

    d_out_part = out_inverse.shape[1]
    in_cols = lax.all_gather(
        lax.dynamic_slice_in_dim(in_inverse, lax.axis_index("fac") * d_out_part, d_out_part, axis=1),
        FSDP,
        axis=0,
        tiled=True,
    )

    gradient, in_cols = lax.optimization_barrier((gradient, in_cols))
    residual = -gradient
    residual_rows = gather_rows(residual)

    gram_cols = d_in // lax.axis_size("fac")
    own_cols = lax.dynamic_slice_in_dim(
        activations, lax.axis_index("fac") * gram_cols, gram_cols, axis=1
    )
    weighted = (own_cols * weights[:, None]).astype(jnp.bfloat16)
    half = gram_cols // 2
    gram_first = block_term(activations, weighted[:, :half], 1.0)
    gram_second = block_term(activations, weighted[:, half:], 1.0)
    residual_rows, first_rows = lax.optimization_barrier((residual_rows, scatter_sum(gram_first)))
    precond = precondition(residual_rows)
    gram_own = jnp.concatenate([first_rows, scatter_sum(gram_second)], axis=1)
    gram_rows = lax.all_gather(gram_own.astype(jnp.bfloat16), "fac", axis=1, tiled=True)

    def curvature(matrix):
        return add_columns(gram_rows, gather_rows(matrix)) + damping * matrix

    direction = precond
    image = curvature(direction)
    image_rows = gather_rows(image)
    inner_now, energy = global_sums(inner_part(residual, precond), inner_part(direction, image))
    gram_inverse = lax.all_gather(
        add_columns(gram_rows, in_cols).astype(jnp.bfloat16), "fac", axis=1, tiled=True
    )
    alpha = inner_now / energy
    newton_step = alpha * direction
    residual = residual - alpha * image
    next_rows = (
        residual_rows.astype(jnp.float32) - alpha * image_rows.astype(jnp.float32)
    ).astype(jnp.bfloat16)

    rows = in_inverse.shape[0]
    left = jnp.concatenate([in_inverse, gram_inverse], axis=0)
    both = add_columns(left, next_rows).astype(jnp.bfloat16)
    both_out = ring_product(both, out_inverse)
    precond = both_out[:rows]
    precond_image = both_out[rows:] + damping * precond
    inner_next, z_hz, z_hd, d_hz = global_sums(
        inner_part(residual, precond),
        inner_part(precond, precond_image),
        inner_part(precond, image),
        inner_part(direction, precond_image),
    )
    beta = inner_next / inner_now
    direction = precond + beta * direction
    image = precond_image + beta * image
    energy = z_hz + beta * (z_hd + d_hz) + beta * beta * energy
    alpha = inner_next / energy
    newton_step = newton_step + alpha * direction
    residual = residual - alpha * image
    return (newton_step, residual)


def solution(mesh):
    cores = 2
    split = jax.sharding.Mesh(
        mesh.devices.reshape(mesh.shape["fsdp"] // cores, cores, mesh.shape["fac"]),
        ("pairs", "core", "fac"),
    )
    placed = (
        P(FSDP, None),
        P(FSDP, "fac"),
        P(FSDP),
        P(FSDP),
        P(),
        P(FSDP, None),
        P(None, "fac"),
    )
    return jax.shard_map(
        body,
        mesh=split,
        in_specs=placed,
        out_specs=(P(FSDP, "fac"), P(FSDP, "fac")),
        check_vma=False,
    )
```

```python
import math

import jax
import jax.numpy as jnp
from jax import lax
from jax.experimental import pallas as pl
from jax.sharding import PartitionSpec as P

ITERS = 2


damping = 0.3


def add_columns(matrix, piece):
    return jnp.dot(matrix, piece, preferred_element_type=jnp.float32)


def transposed_term(matrix, right):
    return lax.dot_general(
        matrix, right, (((0,), (0,)), ((), ())), preferred_element_type=jnp.float32
    )


FSDP = ("pairs", "core")


def ring_product(piece, right):
    n = lax.axis_size("fac")
    me = lax.axis_index("fac")
    width = piece.shape[1]

    def right_block(k):
        return lax.dynamic_slice_in_dim(right, (k % n) * width, width, axis=0)

    total = add_columns(piece, right_block(me))
    ahead = piece
    behind = piece
    for step in range(1, n // 2 + 1):
        ahead = lax.ppermute(ahead, "fac", [(j, (j + 1) % n) for j in range(n)])
        total = total + add_columns(ahead, right_block(me - step))
        if 2 * step < n:
            behind = lax.ppermute(behind, "fac", [(j, (j - 1) % n) for j in range(n)])
            total = total + add_columns(behind, right_block(me + step))
    return total


def block_term(activations, right, scale):
    pairs, cores = lax.axis_size("pairs"), lax.axis_size("core")
    tokens, d_in = activations.shape
    rows = d_in // (pairs * cores)
    cols = right.shape[1]
    step = 384 if cols % 384 == 0 else cols

    def kernel(a_ref, x_ref, o_ref):
        product = lax.dot_general(
            a_ref[...], x_ref[...], (((0,), (0,)), ((), ())), preferred_element_type=jnp.float32
        )
        product = (product * scale).astype(o_ref.dtype)
        for block in range(pairs * cores):
            o_ref[block % cores, block // cores] = product[block * rows : (block + 1) * rows]

    return pl.pallas_call(
        kernel,
        grid=(cols // step,),
        in_specs=[
            pl.BlockSpec((tokens, d_in), lambda j: (0, 0)),
            pl.BlockSpec((tokens, step), lambda j: (0, j)),
        ],
        out_specs=pl.BlockSpec((cores, pairs, rows, step), lambda j: (0, 0, 0, j)),
        out_shape=jax.ShapeDtypeStruct((cores, pairs, rows, cols), jnp.bfloat16),
    )(activations, right)


def scatter_sum(blocks):
    on_chip = lax.all_to_all(blocks, "core", 0, 0, tiled=False)
    chip_sum = jnp.sum(on_chip.astype(jnp.float32), axis=0).astype(jnp.bfloat16)
    received = lax.all_to_all(chip_sum, "pairs", 0, 0, tiled=False)
    return lax.optimization_barrier(jnp.sum(received.astype(jnp.float32), axis=0))


def global_sums(*partials):
    devices = lax.axis_size("pairs") * lax.axis_size("core") * lax.axis_size("fac")
    stacked = jnp.broadcast_to(jnp.stack(partials)[None, :], (devices, len(partials)))
    received = lax.all_to_all(stacked, FSDP + ("fac",), 0, 0, tiled=True)
    total = jnp.sum(received, axis=0)
    return tuple(total[i] for i in range(len(partials)))


def body(activations, out_grads, token_ids, forget_mask, importance, in_inverse, out_inverse):
    tok_rows, d_in = activations.shape
    total = tok_rows * lax.axis_size("pairs") * lax.axis_size("core")
    keep = 1.0 - forget_mask.astype(jnp.float32)
    lanes = 128
    table_rows = importance.reshape(importance.shape[0] // lanes, lanes)[token_ids // lanes]
    lane_ids = lax.broadcasted_iota(jnp.int32, table_rows.shape, 1)
    picked = jnp.sum(
        jnp.where(lane_ids == (token_ids % lanes)[:, None], table_rows, 0.0), axis=1
    )
    weights = picked * keep / total
    forget_grads = out_grads * forget_mask.astype(jnp.bfloat16)[:, None]
    grad_scale = 1.0 / math.sqrt(total)

    gradient = scatter_sum(block_term(activations, forget_grads, grad_scale))

    def gather_rows(matrix):
        return lax.all_gather(matrix.astype(jnp.bfloat16), FSDP, axis=0, tiled=True)

    def precondition(gathered):
        mixed = add_columns(in_inverse, gathered)
        return ring_product(mixed.astype(jnp.bfloat16), out_inverse)

    def inner_part(left, right):
        return jnp.sum(left * right)

    d_out_part = out_inverse.shape[1]
    in_cols = lax.all_gather(
        lax.dynamic_slice_in_dim(in_inverse, lax.axis_index("fac") * d_out_part, d_out_part, axis=1),
        FSDP,
        axis=0,
        tiled=True,
    )

    gradient, in_cols = lax.optimization_barrier((gradient, in_cols))
    residual = -gradient
    residual_rows = gather_rows(residual)

    gram_cols = d_in // lax.axis_size("fac")
    own_cols = lax.dynamic_slice_in_dim(
        activations, lax.axis_index("fac") * gram_cols, gram_cols, axis=1
    )
    weighted = (own_cols * weights[:, None]).astype(jnp.bfloat16)
    half = gram_cols // 2
    gram_first = block_term(activations, weighted[:, :half], 1.0)
    gram_second = block_term(activations, weighted[:, half:], 1.0)
    residual_rows, first_rows = lax.optimization_barrier((residual_rows, scatter_sum(gram_first)))
    precond = precondition(residual_rows)
    gram_own = jnp.concatenate([first_rows, scatter_sum(gram_second)], axis=1).astype(jnp.bfloat16)

    direction = precond
    d_out_part = out_inverse.shape[1]
    gram_both = ring_product(gram_own, jnp.concatenate([gather_rows(direction), in_cols], axis=1))
    image = gram_both[:, :d_out_part] + damping * direction
    image_rows = gather_rows(image)
    inner_now, energy = global_sums(inner_part(residual, precond), inner_part(direction, image))
    gram_inverse = lax.all_gather(
        gram_both[:, d_out_part:].astype(jnp.bfloat16), "fac", axis=1, tiled=True
    )
    alpha = inner_now / energy
    newton_step = alpha * direction
    residual = residual - alpha * image
    next_rows = (
        residual_rows.astype(jnp.float32) - alpha * image_rows.astype(jnp.float32)
    ).astype(jnp.bfloat16)

    rows = in_inverse.shape[0]
    left = jnp.concatenate([in_inverse, gram_inverse], axis=0)
    both = add_columns(left, next_rows).astype(jnp.bfloat16)
    both_out = ring_product(both, out_inverse)
    precond = both_out[:rows]
    precond_image = both_out[rows:] + damping * precond
    inner_next, z_hz, z_hd, d_hz = global_sums(
        inner_part(residual, precond),
        inner_part(precond, precond_image),
        inner_part(precond, image),
        inner_part(direction, precond_image),
    )
    beta = inner_next / inner_now
    direction = precond + beta * direction
    image = precond_image + beta * image
    energy = z_hz + beta * (z_hd + d_hz) + beta * beta * energy
    alpha = inner_next / energy
    newton_step = newton_step + alpha * direction
    residual = residual - alpha * image
    return (newton_step, residual)


def solution(mesh):
    cores = 2
    split = jax.sharding.Mesh(
        mesh.devices.reshape(mesh.shape["fsdp"] // cores, cores, mesh.shape["fac"]),
        ("pairs", "core", "fac"),
    )
    placed = (
        P(FSDP, None),
        P(FSDP, "fac"),
        P(FSDP),
        P(FSDP),
        P(),
        P(FSDP, None),
        P(None, "fac"),
    )
    return jax.shard_map(
        body,
        mesh=split,
        in_specs=placed,
        out_specs=(P(FSDP, "fac"), P(FSDP, "fac")),
        check_vma=False,
    )
```

```python
import math

import jax
import jax.numpy as jnp
from jax import lax
from jax.experimental import pallas as pl
from jax.sharding import PartitionSpec as P

ITERS = 2


damping = 0.3


def add_columns(matrix, piece):
    return jnp.dot(matrix, piece, preferred_element_type=jnp.float32)


def transposed_term(matrix, right):
    return lax.dot_general(
        matrix, right, (((0,), (0,)), ((), ())), preferred_element_type=jnp.float32
    )


FSDP = ("pairs", "core")


def ring_product(piece, right):
    n = lax.axis_size("fac")
    me = lax.axis_index("fac")
    width = piece.shape[1]

    def right_block(k):
        return lax.dynamic_slice_in_dim(right, (k % n) * width, width, axis=0)

    total = add_columns(piece, right_block(me))
    ahead = piece
    behind = piece
    for step in range(1, n // 2 + 1):
        ahead = lax.ppermute(ahead, "fac", [(j, (j + 1) % n) for j in range(n)])
        total = total + add_columns(ahead, right_block(me - step))
        if 2 * step < n:
            behind = lax.ppermute(behind, "fac", [(j, (j - 1) % n) for j in range(n)])
            total = total + add_columns(behind, right_block(me + step))
    return total


def block_term(activations, right, scale):
    pairs, cores = lax.axis_size("pairs"), lax.axis_size("core")
    tokens, d_in = activations.shape
    rows = d_in // (pairs * cores)
    cols = right.shape[1]
    step = 384 if cols % 384 == 0 else cols

    def kernel(a_ref, x_ref, o_ref):
        product = lax.dot_general(
            a_ref[...], x_ref[...], (((0,), (0,)), ((), ())), preferred_element_type=jnp.float32
        )
        product = (product * scale).astype(o_ref.dtype)
        for block in range(pairs * cores):
            o_ref[block % cores, block // cores] = product[block * rows : (block + 1) * rows]

    return pl.pallas_call(
        kernel,
        grid=(cols // step,),
        in_specs=[
            pl.BlockSpec((tokens, d_in), lambda j: (0, 0)),
            pl.BlockSpec((tokens, step), lambda j: (0, j)),
        ],
        out_specs=pl.BlockSpec((cores, pairs, rows, step), lambda j: (0, 0, 0, j)),
        out_shape=jax.ShapeDtypeStruct((cores, pairs, rows, cols), jnp.bfloat16),
    )(activations, right)


def scatter_sum(blocks):
    cores = lax.axis_size("core")
    me = lax.axis_index("core")
    sibling = [(j, (j + 1) % cores) for j in range(cores)]
    sent = lax.ppermute(lax.dynamic_index_in_dim(blocks, 1 - me, 0, keepdims=False), "core", sibling)
    own = lax.dynamic_index_in_dim(blocks, me, 0, keepdims=False)
    chip_sum = (own.astype(jnp.float32) + sent.astype(jnp.float32)).astype(jnp.bfloat16)
    received = lax.all_to_all(chip_sum, "pairs", 0, 0, tiled=False)
    return lax.optimization_barrier(jnp.sum(received.astype(jnp.float32), axis=0))


def global_sums(*partials):
    devices = lax.axis_size("pairs") * lax.axis_size("core") * lax.axis_size("fac")
    stacked = jnp.broadcast_to(jnp.stack(partials)[None, :], (devices, len(partials)))
    received = lax.all_to_all(stacked, FSDP + ("fac",), 0, 0, tiled=True)
    total = jnp.sum(received, axis=0)
    return tuple(total[i] for i in range(len(partials)))


def body(activations, out_grads, token_ids, forget_mask, importance, in_inverse, out_inverse):
    tok_rows, d_in = activations.shape
    total = tok_rows * lax.axis_size("pairs") * lax.axis_size("core")
    keep = 1.0 - forget_mask.astype(jnp.float32)
    lanes = 128
    table_rows = importance.reshape(importance.shape[0] // lanes, lanes)[token_ids // lanes]
    lane_ids = lax.broadcasted_iota(jnp.int32, table_rows.shape, 1)
    picked = jnp.sum(
        jnp.where(lane_ids == (token_ids % lanes)[:, None], table_rows, 0.0), axis=1
    )
    weights = picked * keep / total
    forget_grads = out_grads * forget_mask.astype(jnp.bfloat16)[:, None]
    grad_scale = 1.0 / math.sqrt(total)

    gradient = scatter_sum(block_term(activations, forget_grads, grad_scale))

    def gather_rows(matrix):
        return lax.all_gather(matrix.astype(jnp.bfloat16), FSDP, axis=0, tiled=True)

    def precondition(gathered):
        mixed = add_columns(in_inverse, gathered)
        mixed_low = mixed.astype(jnp.bfloat16)
        return jnp.dot(
            lax.all_gather(mixed_low, "fac", axis=1, tiled=True),
            out_inverse,
            preferred_element_type=jnp.float32,
        )

    def inner_part(left, right):
        return jnp.sum(left * right)

    d_out_part = out_inverse.shape[1]
    in_cols = lax.all_gather(
        lax.dynamic_slice_in_dim(in_inverse, lax.axis_index("fac") * d_out_part, d_out_part, axis=1),
        FSDP,
        axis=0,
        tiled=True,
    )

    gradient, in_cols = lax.optimization_barrier((gradient, in_cols))
    residual = -gradient
    residual_rows = gather_rows(residual)

    gram_cols = d_in // lax.axis_size("fac")
    own_cols = lax.dynamic_slice_in_dim(
        activations, lax.axis_index("fac") * gram_cols, gram_cols, axis=1
    )
    weighted = (own_cols * weights[:, None]).astype(jnp.bfloat16)
    half = gram_cols // 2
    gram_first = block_term(activations, weighted[:, :half], 1.0)
    gram_second = block_term(activations, weighted[:, half:], 1.0)
    residual_rows, first_rows = lax.optimization_barrier((residual_rows, scatter_sum(gram_first)))
    precond = precondition(residual_rows)
    gram_own = jnp.concatenate([first_rows, scatter_sum(gram_second)], axis=1)
    gram_rows = lax.all_gather(gram_own.astype(jnp.bfloat16), "fac", axis=1, tiled=True)

    def curvature(matrix):
        return add_columns(gram_rows, gather_rows(matrix)) + damping * matrix

    direction = precond
    image = curvature(direction)
    image_rows = gather_rows(image)
    inner_now, energy = global_sums(inner_part(residual, precond), inner_part(direction, image))
    gram_inverse = lax.all_gather(
        add_columns(gram_rows, in_cols).astype(jnp.bfloat16), "fac", axis=1, tiled=True
    )
    alpha = inner_now / energy
    newton_step = alpha * direction
    residual = residual - alpha * image
    next_rows = (
        residual_rows.astype(jnp.float32) - alpha * image_rows.astype(jnp.float32)
    ).astype(jnp.bfloat16)

    rows = in_inverse.shape[0]
    left = jnp.concatenate([in_inverse, gram_inverse], axis=0)
    both = add_columns(left, next_rows).astype(jnp.bfloat16)
    both_out = ring_product(both, out_inverse)
    precond = both_out[:rows]
    precond_image = both_out[rows:] + damping * precond
    inner_next, z_hz, z_hd, d_hz = global_sums(
        inner_part(residual, precond),
        inner_part(precond, precond_image),
        inner_part(precond, image),
        inner_part(direction, precond_image),
    )
    beta = inner_next / inner_now
    direction = precond + beta * direction
    image = precond_image + beta * image
    energy = z_hz + beta * (z_hd + d_hz) + beta * beta * energy
    alpha = inner_next / energy
    newton_step = newton_step + alpha * direction
    residual = residual - alpha * image
    return (newton_step, residual)


def solution(mesh):
    cores = 2
    split = jax.sharding.Mesh(
        mesh.devices.reshape(mesh.shape["fsdp"] // cores, cores, mesh.shape["fac"]),
        ("pairs", "core", "fac"),
    )
    placed = (
        P(FSDP, None),
        P(FSDP, "fac"),
        P(FSDP),
        P(FSDP),
        P(),
        P(FSDP, None),
        P(None, "fac"),
    )
    return jax.shard_map(
        body,
        mesh=split,
        in_specs=placed,
        out_specs=(P(FSDP, "fac"), P(FSDP, "fac")),
        check_vma=False,
    )
```

```python
import math

import jax
import jax.numpy as jnp
from jax import lax
from jax.experimental import pallas as pl
from jax.sharding import PartitionSpec as P

ITERS = 2


damping = 0.3


def add_columns(matrix, piece):
    return jnp.dot(matrix, piece, preferred_element_type=jnp.float32)


def transposed_term(matrix, right):
    return lax.dot_general(
        matrix, right, (((0,), (0,)), ((), ())), preferred_element_type=jnp.float32
    )


FSDP = ("pairs", "core")


def ring_product(piece, right):
    n = lax.axis_size("fac")
    me = lax.axis_index("fac")
    width = piece.shape[1]

    def right_block(k):
        return lax.dynamic_slice_in_dim(right, (k % n) * width, width, axis=0)

    total = add_columns(piece, right_block(me))
    ahead = piece
    behind = piece
    for step in range(1, n // 2 + 1):
        ahead = lax.ppermute(ahead, "fac", [(j, (j + 1) % n) for j in range(n)])
        total = total + add_columns(ahead, right_block(me - step))
        if 2 * step < n:
            behind = lax.ppermute(behind, "fac", [(j, (j - 1) % n) for j in range(n)])
            total = total + add_columns(behind, right_block(me + step))
    return total


def block_term(activations, right, factor, scale):
    pairs, cores = lax.axis_size("pairs"), lax.axis_size("core")
    tokens, d_in = activations.shape
    rows = d_in // (pairs * cores)
    cols = right.shape[1]
    step = 384 if cols % 384 == 0 else cols

    def kernel(a_ref, x_ref, f_ref, o_ref):
        scaled = (x_ref[...].astype(jnp.float32) * f_ref[...]).astype(jnp.bfloat16)
        product = lax.dot_general(
            a_ref[...], scaled, (((0,), (0,)), ((), ())), preferred_element_type=jnp.float32
        )
        product = (product * scale).astype(o_ref.dtype)
        for block in range(pairs * cores):
            o_ref[block % cores, block // cores] = product[block * rows : (block + 1) * rows]

    return pl.pallas_call(
        kernel,
        grid=(cols // step,),
        in_specs=[
            pl.BlockSpec((tokens, d_in), lambda j: (0, 0)),
            pl.BlockSpec((tokens, step), lambda j: (0, j)),
            pl.BlockSpec((tokens, 1), lambda j: (0, 0)),
        ],
        out_specs=pl.BlockSpec((cores, pairs, rows, step), lambda j: (0, 0, 0, j)),
        out_shape=jax.ShapeDtypeStruct((cores, pairs, rows, cols), jnp.bfloat16),
    )(activations, right, factor.reshape(tokens, 1))


def scatter_sum(blocks):
    cores = lax.axis_size("core")
    me = lax.axis_index("core")
    sibling = [(j, (j + 1) % cores) for j in range(cores)]
    sent = lax.ppermute(lax.dynamic_index_in_dim(blocks, 1 - me, 0, keepdims=False), "core", sibling)
    own = lax.dynamic_index_in_dim(blocks, me, 0, keepdims=False)
    chip_sum = (own.astype(jnp.float32) + sent.astype(jnp.float32)).astype(jnp.bfloat16)
    received = lax.all_to_all(chip_sum, "pairs", 0, 0, tiled=False)
    return lax.optimization_barrier(jnp.sum(received.astype(jnp.float32), axis=0))


def global_sums(*partials):
    devices = lax.axis_size("pairs") * lax.axis_size("core") * lax.axis_size("fac")
    stacked = jnp.broadcast_to(jnp.stack(partials)[None, :], (devices, len(partials)))
    received = lax.all_to_all(stacked, FSDP + ("fac",), 0, 0, tiled=True)
    total = jnp.sum(received, axis=0)
    return tuple(total[i] for i in range(len(partials)))


def body(activations, out_grads, token_ids, forget_mask, importance, in_inverse, out_inverse):
    tok_rows, d_in = activations.shape
    total = tok_rows * lax.axis_size("pairs") * lax.axis_size("core")
    keep = 1.0 - forget_mask.astype(jnp.float32)
    lanes = 128
    table_rows = importance.reshape(importance.shape[0] // lanes, lanes)[token_ids // lanes]
    lane_ids = lax.broadcasted_iota(jnp.int32, table_rows.shape, 1)
    picked = jnp.sum(
        jnp.where(lane_ids == (token_ids % lanes)[:, None], table_rows, 0.0), axis=1
    )
    weights = picked * keep / total
    grad_scale = 1.0 / math.sqrt(total)

    gradient = scatter_sum(
        block_term(activations, out_grads, forget_mask.astype(jnp.float32), grad_scale)
    )

    def gather_rows(matrix):
        return lax.all_gather(matrix.astype(jnp.bfloat16), FSDP, axis=0, tiled=True)

    def precondition(gathered):
        mixed = add_columns(in_inverse, gathered)
        mixed_low = mixed.astype(jnp.bfloat16)
        return jnp.dot(
            lax.all_gather(mixed_low, "fac", axis=1, tiled=True),
            out_inverse,
            preferred_element_type=jnp.float32,
        )

    def inner_part(left, right):
        return jnp.sum(left * right)

    d_out_part = out_inverse.shape[1]
    in_cols = lax.all_gather(
        lax.dynamic_slice_in_dim(in_inverse, lax.axis_index("fac") * d_out_part, d_out_part, axis=1),
        FSDP,
        axis=0,
        tiled=True,
    )

    gradient, in_cols = lax.optimization_barrier((gradient, in_cols))
    residual = -gradient
    residual_rows = gather_rows(residual)

    gram_cols = d_in // lax.axis_size("fac")
    own_cols = lax.dynamic_slice_in_dim(
        activations, lax.axis_index("fac") * gram_cols, gram_cols, axis=1
    )
    half = gram_cols // 2
    gram_first = block_term(activations, own_cols[:, :half], weights, 1.0)
    gram_second = block_term(activations, own_cols[:, half:], weights, 1.0)
    residual_rows, first_rows = lax.optimization_barrier((residual_rows, scatter_sum(gram_first)))
    precond = precondition(residual_rows)
    gram_own = jnp.concatenate([first_rows, scatter_sum(gram_second)], axis=1)
    gram_rows = lax.all_gather(gram_own.astype(jnp.bfloat16), "fac", axis=1, tiled=True)

    def curvature(matrix):
        return add_columns(gram_rows, gather_rows(matrix)) + damping * matrix

    direction = precond
    image = curvature(direction)
    image_rows = gather_rows(image)
    inner_now, energy = global_sums(inner_part(residual, precond), inner_part(direction, image))
    gram_inverse = lax.all_gather(
        add_columns(gram_rows, in_cols).astype(jnp.bfloat16), "fac", axis=1, tiled=True
    )
    alpha = inner_now / energy
    newton_step = alpha * direction
    residual = residual - alpha * image
    next_rows = (
        residual_rows.astype(jnp.float32) - alpha * image_rows.astype(jnp.float32)
    ).astype(jnp.bfloat16)

    rows = in_inverse.shape[0]
    left = jnp.concatenate([in_inverse, gram_inverse], axis=0)
    both = add_columns(left, next_rows).astype(jnp.bfloat16)
    both_out = ring_product(both, out_inverse)
    precond = both_out[:rows]
    precond_image = both_out[rows:] + damping * precond
    inner_next, z_hz, z_hd, d_hz = global_sums(
        inner_part(residual, precond),
        inner_part(precond, precond_image),
        inner_part(precond, image),
        inner_part(direction, precond_image),
    )
    beta = inner_next / inner_now
    direction = precond + beta * direction
    image = precond_image + beta * image
    energy = z_hz + beta * (z_hd + d_hz) + beta * beta * energy
    alpha = inner_next / energy
    newton_step = newton_step + alpha * direction
    residual = residual - alpha * image
    return (newton_step, residual)


def solution(mesh):
    cores = 2
    split = jax.sharding.Mesh(
        mesh.devices.reshape(mesh.shape["fsdp"] // cores, cores, mesh.shape["fac"]),
        ("pairs", "core", "fac"),
    )
    placed = (
        P(FSDP, None),
        P(FSDP, "fac"),
        P(FSDP),
        P(FSDP),
        P(),
        P(FSDP, None),
        P(None, "fac"),
    )
    return jax.shard_map(
        body,
        mesh=split,
        in_specs=placed,
        out_specs=(P(FSDP, "fac"), P(FSDP, "fac")),
        check_vma=False,
    )
```

```python
import math

import jax
import jax.numpy as jnp
from jax import lax
from jax.experimental import pallas as pl
from jax.experimental.pallas import tpu as pltpu
from jax.sharding import PartitionSpec as P

ITERS = 2


damping = 0.3


def add_columns(matrix, piece):
    return jnp.dot(matrix, piece, preferred_element_type=jnp.float32)


def transposed_term(matrix, right):
    return lax.dot_general(
        matrix, right, (((0,), (0,)), ((), ())), preferred_element_type=jnp.float32
    )


FSDP = ("pairs", "core")


def ring_product(piece, right):
    n = lax.axis_size("fac")
    me = lax.axis_index("fac")
    width = piece.shape[1]

    def right_block(k):
        return lax.dynamic_slice_in_dim(right, (k % n) * width, width, axis=0)

    total = add_columns(piece, right_block(me))
    ahead = piece
    behind = piece
    for step in range(1, n // 2 + 1):
        ahead = lax.ppermute(ahead, "fac", [(j, (j + 1) % n) for j in range(n)])
        total = total + add_columns(ahead, right_block(me - step))
        if 2 * step < n:
            behind = lax.ppermute(behind, "fac", [(j, (j - 1) % n) for j in range(n)])
            total = total + add_columns(behind, right_block(me + step))
    return total


def block_term(activations, right, factor, scale):
    pairs, cores = lax.axis_size("pairs"), lax.axis_size("core")
    tokens, d_in = activations.shape
    rows = d_in // (pairs * cores)
    cols = right.shape[1]
    step = 384 if cols % 384 == 0 else cols

    def kernel(a_ref, x_ref, f_ref, own_ref, other_ref, product_ref):
        scaled = (x_ref[...].astype(jnp.float32) * f_ref[...]).astype(jnp.bfloat16)
        product = lax.dot_general(
            a_ref[...], scaled, (((0,), (0,)), ((), ())), preferred_element_type=jnp.float32
        )
        product_ref[...] = (product * scale).astype(product_ref.dtype)
        me = lax.axis_index("core")
        for pair in range(pairs):
            mine = pl.multiple_of((pair * cores + me) * rows, rows)
            theirs = pl.multiple_of((pair * cores + (cores - 1 - me)) * rows, rows)
            own_ref[pair] = product_ref[pl.ds(mine, rows), :]
            other_ref[pair] = product_ref[pl.ds(theirs, rows), :]

    half = jax.ShapeDtypeStruct((pairs, rows, cols), jnp.bfloat16)
    return pl.pallas_call(
        kernel,
        grid=(cols // step,),
        in_specs=[
            pl.BlockSpec((tokens, d_in), lambda j: (0, 0)),
            pl.BlockSpec((tokens, step), lambda j: (0, j)),
            pl.BlockSpec((tokens, 1), lambda j: (0, 0)),
        ],
        out_specs=[
            pl.BlockSpec((pairs, rows, step), lambda j: (0, 0, j)),
            pl.BlockSpec((pairs, rows, step), lambda j: (0, 0, j)),
        ],
        out_shape=[half, half],
        scratch_shapes=[pltpu.VMEM((d_in, step), jnp.bfloat16)],
    )(activations, right, factor.reshape(tokens, 1))


def scatter_sum(halves):
    cores = lax.axis_size("core")
    own, other = halves
    sibling = [(j, (j + 1) % cores) for j in range(cores)]
    sent = lax.ppermute(other, "core", sibling)
    chip_sum = (own.astype(jnp.float32) + sent.astype(jnp.float32)).astype(jnp.bfloat16)
    received = lax.all_to_all(chip_sum, "pairs", 0, 0, tiled=False)
    return lax.optimization_barrier(jnp.sum(received.astype(jnp.float32), axis=0))


def global_sums(*partials):
    devices = lax.axis_size("pairs") * lax.axis_size("core") * lax.axis_size("fac")
    stacked = jnp.broadcast_to(jnp.stack(partials)[None, :], (devices, len(partials)))
    received = lax.all_to_all(stacked, FSDP + ("fac",), 0, 0, tiled=True)
    total = jnp.sum(received, axis=0)
    return tuple(total[i] for i in range(len(partials)))


def body(activations, out_grads, token_ids, forget_mask, importance, in_inverse, out_inverse):
    tok_rows, d_in = activations.shape
    total = tok_rows * lax.axis_size("pairs") * lax.axis_size("core")
    keep = 1.0 - forget_mask.astype(jnp.float32)
    lanes = 128
    table_rows = importance.reshape(importance.shape[0] // lanes, lanes)[token_ids // lanes]
    lane_ids = lax.broadcasted_iota(jnp.int32, table_rows.shape, 1)
    picked = jnp.sum(
        jnp.where(lane_ids == (token_ids % lanes)[:, None], table_rows, 0.0), axis=1
    )
    weights = picked * keep / total
    grad_scale = 1.0 / math.sqrt(total)

    gradient = scatter_sum(
        block_term(activations, out_grads, forget_mask.astype(jnp.float32), grad_scale)
    )

    def gather_rows(matrix):
        return lax.all_gather(matrix.astype(jnp.bfloat16), FSDP, axis=0, tiled=True)

    def precondition(gathered):
        mixed = add_columns(in_inverse, gathered)
        mixed_low = mixed.astype(jnp.bfloat16)
        return jnp.dot(
            lax.all_gather(mixed_low, "fac", axis=1, tiled=True),
            out_inverse,
            preferred_element_type=jnp.float32,
        )

    def inner_part(left, right):
        return jnp.sum(left * right)

    d_out_part = out_inverse.shape[1]
    in_cols = lax.all_gather(
        lax.dynamic_slice_in_dim(in_inverse, lax.axis_index("fac") * d_out_part, d_out_part, axis=1),
        FSDP,
        axis=0,
        tiled=True,
    )

    gradient, in_cols = lax.optimization_barrier((gradient, in_cols))
    residual = -gradient
    residual_rows = gather_rows(residual)

    gram_cols = d_in // lax.axis_size("fac")
    own_cols = lax.dynamic_slice_in_dim(
        activations, lax.axis_index("fac") * gram_cols, gram_cols, axis=1
    )
    half = gram_cols // 2
    gram_first = block_term(activations, own_cols[:, :half], weights, 1.0)
    gram_second = block_term(activations, own_cols[:, half:], weights, 1.0)
    residual_rows, first_rows = lax.optimization_barrier((residual_rows, scatter_sum(gram_first)))
    precond = precondition(residual_rows)
    gram_own = jnp.concatenate([first_rows, scatter_sum(gram_second)], axis=1)
    gram_rows = lax.all_gather(gram_own.astype(jnp.bfloat16), "fac", axis=1, tiled=True)

    def curvature(matrix):
        return add_columns(gram_rows, gather_rows(matrix)) + damping * matrix

    direction = precond
    image = curvature(direction)
    image_rows = gather_rows(image)
    inner_now, energy = global_sums(inner_part(residual, precond), inner_part(direction, image))
    gram_inverse = lax.all_gather(
        add_columns(gram_rows, in_cols).astype(jnp.bfloat16), "fac", axis=1, tiled=True
    )
    alpha = inner_now / energy
    newton_step = alpha * direction
    residual = residual - alpha * image
    next_rows = (
        residual_rows.astype(jnp.float32) - alpha * image_rows.astype(jnp.float32)
    ).astype(jnp.bfloat16)

    rows = in_inverse.shape[0]
    left = jnp.concatenate([in_inverse, gram_inverse], axis=0)
    both = add_columns(left, next_rows).astype(jnp.bfloat16)
    both_out = ring_product(both, out_inverse)
    precond = both_out[:rows]
    precond_image = both_out[rows:] + damping * precond
    inner_next, z_hz, z_hd, d_hz = global_sums(
        inner_part(residual, precond),
        inner_part(precond, precond_image),
        inner_part(precond, image),
        inner_part(direction, precond_image),
    )
    beta = inner_next / inner_now
    direction = precond + beta * direction
    image = precond_image + beta * image
    energy = z_hz + beta * (z_hd + d_hz) + beta * beta * energy
    alpha = inner_next / energy
    newton_step = newton_step + alpha * direction
    residual = residual - alpha * image
    return (newton_step, residual)


def solution(mesh):
    cores = 2
    split = jax.sharding.Mesh(
        mesh.devices.reshape(mesh.shape["fsdp"] // cores, cores, mesh.shape["fac"]),
        ("pairs", "core", "fac"),
    )
    placed = (
        P(FSDP, None),
        P(FSDP, "fac"),
        P(FSDP),
        P(FSDP),
        P(),
        P(FSDP, None),
        P(None, "fac"),
    )
    return jax.shard_map(
        body,
        mesh=split,
        in_specs=placed,
        out_specs=(P(FSDP, "fac"), P(FSDP, "fac")),
        check_vma=False,
    )
```

```python
import math

import jax
import jax.numpy as jnp
from jax import lax
from jax.experimental import pallas as pl
from jax.sharding import PartitionSpec as P

ITERS = 2


damping = 0.3


def add_columns(matrix, piece):
    return jnp.dot(matrix, piece, preferred_element_type=jnp.float32)


def transposed_term(matrix, right):
    return lax.dot_general(
        matrix, right, (((0,), (0,)), ((), ())), preferred_element_type=jnp.float32
    )


FSDP = ("pairs", "core")


def ring_product(piece, right):
    n = lax.axis_size("fac")
    me = lax.axis_index("fac")
    width = piece.shape[1]

    def right_block(k):
        return lax.dynamic_slice_in_dim(right, (k % n) * width, width, axis=0)

    total = add_columns(piece, right_block(me))
    ahead = piece
    behind = piece
    for step in range(1, n // 2 + 1):
        ahead = lax.ppermute(ahead, "fac", [(j, (j + 1) % n) for j in range(n)])
        total = total + add_columns(ahead, right_block(me - step))
        if 2 * step < n:
            behind = lax.ppermute(behind, "fac", [(j, (j - 1) % n) for j in range(n)])
            total = total + add_columns(behind, right_block(me + step))
    return total


def block_term(activations, right, factor, scale):
    pairs, cores = lax.axis_size("pairs"), lax.axis_size("core")
    tokens, d_in = activations.shape
    rows = d_in // (pairs * cores)
    cols = right.shape[1]
    step = 384 if cols % 384 == 0 else cols

    def kernel(a_ref, x_ref, f_ref, o_ref):
        scaled = (x_ref[...].astype(jnp.float32) * f_ref[...]).astype(jnp.bfloat16)
        product = lax.dot_general(
            a_ref[...], scaled, (((0,), (0,)), ((), ())), preferred_element_type=jnp.float32
        )
        product = (product * scale).astype(o_ref.dtype)
        for block in range(pairs * cores):
            o_ref[block % cores, block // cores] = product[block * rows : (block + 1) * rows]

    return pl.pallas_call(
        kernel,
        grid=(cols // step,),
        in_specs=[
            pl.BlockSpec((tokens, d_in), lambda j: (0, 0)),
            pl.BlockSpec((tokens, step), lambda j: (0, j)),
            pl.BlockSpec((tokens, 1), lambda j: (0, 0)),
        ],
        out_specs=pl.BlockSpec((cores, pairs, rows, step), lambda j: (0, 0, 0, j)),
        out_shape=jax.ShapeDtypeStruct((cores, pairs, rows, cols), jnp.bfloat16),
    )(activations, right, factor.reshape(tokens, 1))


def scatter_sum(blocks):
    cores = lax.axis_size("core")
    me = lax.axis_index("core")
    sibling = [(j, (j + 1) % cores) for j in range(cores)]
    sent = lax.ppermute(lax.dynamic_index_in_dim(blocks, 1 - me, 0, keepdims=False), "core", sibling)
    own = lax.dynamic_index_in_dim(blocks, me, 0, keepdims=False)
    chip_sum = (own.astype(jnp.float32) + sent.astype(jnp.float32)).astype(jnp.bfloat16)
    received = lax.all_to_all(chip_sum, "pairs", 0, 0, tiled=False)
    return lax.optimization_barrier(jnp.sum(received.astype(jnp.float32), axis=0))


def global_sums(*partials):
    devices = lax.axis_size("pairs") * lax.axis_size("core") * lax.axis_size("fac")
    stacked = jnp.broadcast_to(jnp.stack(partials)[None, :], (devices, len(partials)))
    received = lax.all_to_all(stacked, FSDP + ("fac",), 0, 0, tiled=True)
    total = jnp.sum(received, axis=0)
    return tuple(total[i] for i in range(len(partials)))


def body(activations, out_grads, token_ids, forget_mask, importance, in_inverse, out_inverse):
    tok_rows, d_in = activations.shape
    total = tok_rows * lax.axis_size("pairs") * lax.axis_size("core")
    keep = 1.0 - forget_mask.astype(jnp.float32)
    lanes = 128
    table_rows = importance.reshape(importance.shape[0] // lanes, lanes)[token_ids // lanes]
    lane_ids = lax.broadcasted_iota(jnp.int32, table_rows.shape, 1)
    picked = jnp.sum(
        jnp.where(lane_ids == (token_ids % lanes)[:, None], table_rows, 0.0), axis=1
    )
    weights = picked * keep / total
    grad_scale = 1.0 / math.sqrt(total)

    gradient = scatter_sum(
        block_term(activations, out_grads, forget_mask.astype(jnp.float32), grad_scale)
    )

    def gather_rows(matrix):
        return lax.all_gather(matrix.astype(jnp.bfloat16), FSDP, axis=0, tiled=True)

    def precondition(gathered):
        mixed = add_columns(in_inverse, gathered)
        mixed_low = mixed.astype(jnp.bfloat16)
        return jnp.dot(
            lax.all_gather(mixed_low, "fac", axis=1, tiled=True),
            out_inverse,
            preferred_element_type=jnp.float32,
        )

    def inner_part(left, right):
        return jnp.sum(left * right)

    d_out_part = out_inverse.shape[1]
    in_cols = lax.all_gather(
        lax.dynamic_slice_in_dim(in_inverse, lax.axis_index("fac") * d_out_part, d_out_part, axis=1),
        FSDP,
        axis=0,
        tiled=True,
    )

    gradient, in_cols = lax.optimization_barrier((gradient, in_cols))
    residual = -gradient
    residual_rows = gather_rows(residual)

    gram_cols = d_in // lax.axis_size("fac")
    own_cols = lax.dynamic_slice_in_dim(
        activations, lax.axis_index("fac") * gram_cols, gram_cols, axis=1
    )
    half = gram_cols // 2
    gram_first = block_term(activations, own_cols[:, :half], weights, 1.0)
    gram_second = block_term(activations, own_cols[:, half:], weights, 1.0)
    residual_rows, first_rows = lax.optimization_barrier((residual_rows, scatter_sum(gram_first)))
    precond = precondition(residual_rows)
    gram_own = jnp.concatenate([first_rows, scatter_sum(gram_second)], axis=1)
    gram_rows = lax.all_gather(gram_own.astype(jnp.bfloat16), "fac", axis=1, tiled=True)

    def curvature(matrix):
        return add_columns(gram_rows, gather_rows(matrix)) + damping * matrix

    direction = precond
    image = curvature(direction)
    image_rows = gather_rows(image)
    inner_now, energy = global_sums(inner_part(residual, precond), inner_part(direction, image))
    gram_inverse = lax.all_gather(
        add_columns(gram_rows, in_cols).astype(jnp.bfloat16), "fac", axis=1, tiled=True
    )
    alpha = inner_now / energy
    newton_step = alpha * direction
    residual = residual - alpha * image
    next_rows = (
        residual_rows.astype(jnp.float32) - alpha * image_rows.astype(jnp.float32)
    ).astype(jnp.bfloat16)

    precond = ring_product(add_columns(in_inverse, next_rows).astype(jnp.bfloat16), out_inverse)
    precond_image = (
        ring_product(add_columns(gram_inverse, next_rows).astype(jnp.bfloat16), out_inverse)
        + damping * precond
    )
    inner_next, z_hz, z_hd, d_hz = global_sums(
        inner_part(residual, precond),
        inner_part(precond, precond_image),
        inner_part(precond, image),
        inner_part(direction, precond_image),
    )
    beta = inner_next / inner_now
    direction = precond + beta * direction
    image = precond_image + beta * image
    energy = z_hz + beta * (z_hd + d_hz) + beta * beta * energy
    alpha = inner_next / energy
    newton_step = newton_step + alpha * direction
    residual = residual - alpha * image
    return (newton_step, residual)


def solution(mesh):
    cores = 2
    split = jax.sharding.Mesh(
        mesh.devices.reshape(mesh.shape["fsdp"] // cores, cores, mesh.shape["fac"]),
        ("pairs", "core", "fac"),
    )
    placed = (
        P(FSDP, None),
        P(FSDP, "fac"),
        P(FSDP),
        P(FSDP),
        P(),
        P(FSDP, None),
        P(None, "fac"),
    )
    return jax.shard_map(
        body,
        mesh=split,
        in_specs=placed,
        out_specs=(P(FSDP, "fac"), P(FSDP, "fac")),
        check_vma=False,
    )
```

```python
import math

import jax
import jax.numpy as jnp
from jax import lax
from jax.experimental import pallas as pl
from jax.sharding import PartitionSpec as P

ITERS = 2


damping = 0.3


def add_columns(matrix, piece):
    return jnp.dot(matrix, piece, preferred_element_type=jnp.float32)


def transposed_term(matrix, right):
    return lax.dot_general(
        matrix, right, (((0,), (0,)), ((), ())), preferred_element_type=jnp.float32
    )


FSDP = ("pairs", "core")


def ring_product(piece, right):
    n = lax.axis_size("fac")
    me = lax.axis_index("fac")
    width = piece.shape[1]

    def right_block(k):
        return lax.dynamic_slice_in_dim(right, (k % n) * width, width, axis=0)

    total = add_columns(piece, right_block(me))
    ahead = piece
    behind = piece
    for step in range(1, n // 2 + 1):
        ahead = lax.ppermute(ahead, "fac", [(j, (j + 1) % n) for j in range(n)])
        total = total + add_columns(ahead, right_block(me - step))
        if 2 * step < n:
            behind = lax.ppermute(behind, "fac", [(j, (j - 1) % n) for j in range(n)])
            total = total + add_columns(behind, right_block(me + step))
    return total


def block_term(activations, right, factor, scale):
    pairs, cores = lax.axis_size("pairs"), lax.axis_size("core")
    tokens, d_in = activations.shape
    rows = d_in // (pairs * cores)
    cols = right.shape[1]
    step = 384 if cols % 384 == 0 else cols

    def kernel(a_ref, x_ref, f_ref, o_ref):
        scaled = (x_ref[...].astype(jnp.float32) * f_ref[...]).astype(jnp.bfloat16)
        product = lax.dot_general(
            a_ref[...], scaled, (((0,), (0,)), ((), ())), preferred_element_type=jnp.float32
        )
        product = (product * scale).astype(o_ref.dtype)
        for block in range(pairs * cores):
            o_ref[block % cores, block // cores] = product[block * rows : (block + 1) * rows]

    return pl.pallas_call(
        kernel,
        grid=(cols // step,),
        in_specs=[
            pl.BlockSpec((tokens, d_in), lambda j: (0, 0)),
            pl.BlockSpec((tokens, step), lambda j: (0, j)),
            pl.BlockSpec((tokens, 1), lambda j: (0, 0)),
        ],
        out_specs=pl.BlockSpec((cores, pairs, rows, step), lambda j: (0, 0, 0, j)),
        out_shape=jax.ShapeDtypeStruct((cores, pairs, rows, cols), jnp.bfloat16),
    )(activations, right, factor.reshape(tokens, 1))


def scatter_sum(blocks):
    cores = lax.axis_size("core")
    me = lax.axis_index("core")
    sibling = [(j, (j + 1) % cores) for j in range(cores)]
    sent = lax.ppermute(lax.dynamic_index_in_dim(blocks, 1 - me, 0, keepdims=False), "core", sibling)
    own = lax.dynamic_index_in_dim(blocks, me, 0, keepdims=False)
    chip_sum = (own.astype(jnp.float32) + sent.astype(jnp.float32)).astype(jnp.bfloat16)
    received = lax.all_to_all(chip_sum, "pairs", 0, 0, tiled=False)
    return lax.optimization_barrier(jnp.sum(received.astype(jnp.float32), axis=0))


def global_sums(*partials):
    devices = lax.axis_size("pairs") * lax.axis_size("core") * lax.axis_size("fac")
    stacked = jnp.broadcast_to(jnp.stack(partials)[None, :], (devices, len(partials)))
    received = lax.all_to_all(stacked, FSDP + ("fac",), 0, 0, tiled=True)
    total = jnp.sum(received, axis=0)
    return tuple(total[i] for i in range(len(partials)))


def body(activations, out_grads, token_ids, forget_mask, importance, in_inverse, out_inverse):
    tok_rows, d_in = activations.shape
    total = tok_rows * lax.axis_size("pairs") * lax.axis_size("core")
    keep = 1.0 - forget_mask.astype(jnp.float32)
    lanes = 128
    table_rows = importance.reshape(importance.shape[0] // lanes, lanes)[token_ids // lanes]
    lane_ids = lax.broadcasted_iota(jnp.int32, table_rows.shape, 1)
    picked = jnp.sum(
        jnp.where(lane_ids == (token_ids % lanes)[:, None], table_rows, 0.0), axis=1
    )
    weights = picked * keep / total
    grad_scale = 1.0 / math.sqrt(total)

    gradient = scatter_sum(
        block_term(activations, out_grads, forget_mask.astype(jnp.float32), grad_scale)
    )

    cores = lax.axis_size("core")
    me = lax.axis_index("core")
    sibling = [(j, (j + 1) % cores) for j in range(cores)]

    def gather_rows(matrix):
        mine = lax.all_gather(matrix.astype(jnp.bfloat16), "pairs", axis=0, tiled=True)
        return mine, lax.ppermute(mine, "core", sibling)

    def split_cols(matrix):
        blocks = matrix.reshape(matrix.shape[0], -1, cores, matrix.shape[1] // (cores * lax.axis_size("pairs")))
        pick = lambda k: lax.dynamic_index_in_dim(blocks, k, 2, keepdims=False).reshape(matrix.shape[0], -1)
        return pick(me), pick(cores - 1 - me)

    def rows_product(left_pair, rows_pair):
        return add_columns(left_pair[0], rows_pair[0]) + add_columns(left_pair[1], rows_pair[1])

    in_pair = split_cols(in_inverse)

    def precondition(gathered):
        mixed = rows_product(in_pair, gathered)
        mixed_low = mixed.astype(jnp.bfloat16)
        return jnp.dot(
            lax.all_gather(mixed_low, "fac", axis=1, tiled=True),
            out_inverse,
            preferred_element_type=jnp.float32,
        )

    def inner_part(left, right):
        return jnp.sum(left * right)

    d_out_part = out_inverse.shape[1]
    in_cols = lax.all_gather(
        lax.dynamic_slice_in_dim(in_inverse, lax.axis_index("fac") * d_out_part, d_out_part, axis=1),
        FSDP,
        axis=0,
        tiled=True,
    )

    gradient, in_cols = lax.optimization_barrier((gradient, in_cols))
    residual = -gradient
    residual_rows = gather_rows(residual)

    gram_cols = d_in // lax.axis_size("fac")
    own_cols = lax.dynamic_slice_in_dim(
        activations, lax.axis_index("fac") * gram_cols, gram_cols, axis=1
    )
    half = gram_cols // 2
    gram_first = block_term(activations, own_cols[:, :half], weights, 1.0)
    gram_second = block_term(activations, own_cols[:, half:], weights, 1.0)
    residual_rows, first_rows = lax.optimization_barrier((residual_rows, scatter_sum(gram_first)))
    precond = precondition(residual_rows)
    gram_own = jnp.concatenate([first_rows, scatter_sum(gram_second)], axis=1)
    gram_rows = lax.all_gather(gram_own.astype(jnp.bfloat16), "fac", axis=1, tiled=True)
    gram_pair = split_cols(gram_rows)

    def curvature(matrix):
        return rows_product(gram_pair, gather_rows(matrix)) + damping * matrix

    direction = precond
    image = curvature(direction)
    image_rows = gather_rows(image)
    inner_now, energy = global_sums(inner_part(residual, precond), inner_part(direction, image))
    gram_inverse = lax.all_gather(
        add_columns(gram_rows, in_cols).astype(jnp.bfloat16), "fac", axis=1, tiled=True
    )
    alpha = inner_now / energy
    newton_step = alpha * direction
    residual = residual - alpha * image
    next_rows = tuple(
        (r.astype(jnp.float32) - alpha * i.astype(jnp.float32)).astype(jnp.bfloat16)
        for r, i in zip(residual_rows, image_rows)
    )

    rows = in_inverse.shape[0]
    left = jnp.concatenate([in_inverse, gram_inverse], axis=0)
    both = rows_product(split_cols(left), next_rows).astype(jnp.bfloat16)
    both_out = ring_product(both, out_inverse)
    precond = both_out[:rows]
    precond_image = both_out[rows:] + damping * precond
    inner_next, z_hz, z_hd, d_hz = global_sums(
        inner_part(residual, precond),
        inner_part(precond, precond_image),
        inner_part(precond, image),
        inner_part(direction, precond_image),
    )
    beta = inner_next / inner_now
    direction = precond + beta * direction
    image = precond_image + beta * image
    energy = z_hz + beta * (z_hd + d_hz) + beta * beta * energy
    alpha = inner_next / energy
    newton_step = newton_step + alpha * direction
    residual = residual - alpha * image
    return (newton_step, residual)


def solution(mesh):
    cores = 2
    split = jax.sharding.Mesh(
        mesh.devices.reshape(mesh.shape["fsdp"] // cores, cores, mesh.shape["fac"]),
        ("pairs", "core", "fac"),
    )
    placed = (
        P(FSDP, None),
        P(FSDP, "fac"),
        P(FSDP),
        P(FSDP),
        P(),
        P(FSDP, None),
        P(None, "fac"),
    )
    return jax.shard_map(
        body,
        mesh=split,
        in_specs=placed,
        out_specs=(P(FSDP, "fac"), P(FSDP, "fac")),
        check_vma=False,
    )
```

```python
import math

import jax
import jax.numpy as jnp
from jax import lax
from jax.experimental import pallas as pl
from jax.sharding import PartitionSpec as P

ITERS = 2


damping = 0.3


def add_columns(matrix, piece):
    return jnp.dot(matrix, piece, preferred_element_type=jnp.float32)


def transposed_term(matrix, right):
    return lax.dot_general(
        matrix, right, (((0,), (0,)), ((), ())), preferred_element_type=jnp.float32
    )


FSDP = ("pairs", "core")


def ring_product(piece, right):
    n = lax.axis_size("fac")
    me = lax.axis_index("fac")
    width = piece.shape[1]

    def right_block(k):
        return lax.dynamic_slice_in_dim(right, (k % n) * width, width, axis=0)

    total = add_columns(piece, right_block(me))
    ahead = piece
    behind = piece
    for step in range(1, n // 2 + 1):
        ahead = lax.ppermute(ahead, "fac", [(j, (j + 1) % n) for j in range(n)])
        total = total + add_columns(ahead, right_block(me - step))
        if 2 * step < n:
            behind = lax.ppermute(behind, "fac", [(j, (j - 1) % n) for j in range(n)])
            total = total + add_columns(behind, right_block(me + step))
    return total


def block_term(activations, right, factor, scale, own_half=None):
    pairs, cores = lax.axis_size("pairs"), lax.axis_size("core")
    tokens, d_in = activations.shape
    rows = d_in // (pairs * cores)
    cols = right.shape[1] if own_half is None else own_half[1]
    step = 384 if cols % 384 == 0 else cols

    def kernel(a_ref, x_ref, f_ref, o_ref):
        if own_half is None:
            x = x_ref[...]
        else:
            start = (lax.axis_index("fac") * 2 + own_half[0]) * cols + pl.program_id(0) * step
            x = a_ref[:, pl.ds(pl.multiple_of(start, 128), step)]
        scaled = (x.astype(jnp.float32) * f_ref[...]).astype(jnp.bfloat16)
        product = lax.dot_general(
            a_ref[...], scaled, (((0,), (0,)), ((), ())), preferred_element_type=jnp.float32
        )
        product = (product * scale).astype(o_ref.dtype)
        for block in range(pairs * cores):
            o_ref[block % cores, block // cores] = product[block * rows : (block + 1) * rows]

    return pl.pallas_call(
        kernel,
        grid=(cols // step,),
        in_specs=[
            pl.BlockSpec((tokens, d_in), lambda j: (0, 0)),
            pl.BlockSpec((tokens, step), lambda j: (0, j if own_half is None else 0)),
            pl.BlockSpec((tokens, 1), lambda j: (0, 0)),
        ],
        out_specs=pl.BlockSpec((cores, pairs, rows, step), lambda j: (0, 0, 0, j)),
        out_shape=jax.ShapeDtypeStruct((cores, pairs, rows, cols), jnp.bfloat16),
    )(activations, right, factor.reshape(tokens, 1))


def scatter_sum(blocks):
    cores = lax.axis_size("core")
    me = lax.axis_index("core")
    sibling = [(j, (j + 1) % cores) for j in range(cores)]
    sent = lax.ppermute(lax.dynamic_index_in_dim(blocks, 1 - me, 0, keepdims=False), "core", sibling)
    own = lax.dynamic_index_in_dim(blocks, me, 0, keepdims=False)
    chip_sum = (own.astype(jnp.float32) + sent.astype(jnp.float32)).astype(jnp.bfloat16)
    received = lax.all_to_all(chip_sum, "pairs", 0, 0, tiled=False)
    return lax.optimization_barrier(jnp.sum(received.astype(jnp.float32), axis=0))


def global_sums(*partials):
    devices = lax.axis_size("pairs") * lax.axis_size("core") * lax.axis_size("fac")
    stacked = jnp.broadcast_to(jnp.stack(partials)[None, :], (devices, len(partials)))
    received = lax.all_to_all(stacked, FSDP + ("fac",), 0, 0, tiled=True)
    total = jnp.sum(received, axis=0)
    return tuple(total[i] for i in range(len(partials)))


def body(activations, out_grads, token_ids, forget_mask, importance, in_inverse, out_inverse):
    tok_rows, d_in = activations.shape
    total = tok_rows * lax.axis_size("pairs") * lax.axis_size("core")
    keep = 1.0 - forget_mask.astype(jnp.float32)
    lanes = 128
    table_rows = importance.reshape(importance.shape[0] // lanes, lanes)[token_ids // lanes]
    lane_ids = lax.broadcasted_iota(jnp.int32, table_rows.shape, 1)
    picked = jnp.sum(
        jnp.where(lane_ids == (token_ids % lanes)[:, None], table_rows, 0.0), axis=1
    )
    weights = picked * keep / total
    grad_scale = 1.0 / math.sqrt(total)

    gradient = scatter_sum(
        block_term(activations, out_grads, forget_mask.astype(jnp.float32), grad_scale)
    )

    def gather_rows(matrix):
        return lax.all_gather(matrix.astype(jnp.bfloat16), FSDP, axis=0, tiled=True)

    def precondition(gathered):
        mixed = add_columns(in_inverse, gathered)
        mixed_low = mixed.astype(jnp.bfloat16)
        return jnp.dot(
            lax.all_gather(mixed_low, "fac", axis=1, tiled=True),
            out_inverse,
            preferred_element_type=jnp.float32,
        )

    def inner_part(left, right):
        return jnp.sum(left * right)

    d_out_part = out_inverse.shape[1]
    in_cols = lax.all_gather(
        lax.dynamic_slice_in_dim(in_inverse, lax.axis_index("fac") * d_out_part, d_out_part, axis=1),
        FSDP,
        axis=0,
        tiled=True,
    )

    gradient, in_cols = lax.optimization_barrier((gradient, in_cols))
    residual = -gradient
    residual_rows = gather_rows(residual)

    gram_cols = d_in // lax.axis_size("fac")
    half = gram_cols // 2
    gram_first = block_term(activations, activations, weights, 1.0, own_half=(0, half))
    gram_second = block_term(activations, activations, weights, 1.0, own_half=(1, half))
    residual_rows, first_rows = lax.optimization_barrier((residual_rows, scatter_sum(gram_first)))
    precond = precondition(residual_rows)
    gram_own = jnp.concatenate([first_rows, scatter_sum(gram_second)], axis=1)
    gram_rows = lax.all_gather(gram_own.astype(jnp.bfloat16), "fac", axis=1, tiled=True)

    def curvature(matrix):
        return add_columns(gram_rows, gather_rows(matrix)) + damping * matrix

    direction = precond
    image = curvature(direction)
    image_rows = gather_rows(image)
    inner_now, energy = global_sums(inner_part(residual, precond), inner_part(direction, image))
    gram_inverse = lax.all_gather(
        add_columns(gram_rows, in_cols).astype(jnp.bfloat16), "fac", axis=1, tiled=True
    )
    alpha = inner_now / energy
    newton_step = alpha * direction
    residual = residual - alpha * image
    next_rows = (
        residual_rows.astype(jnp.float32) - alpha * image_rows.astype(jnp.float32)
    ).astype(jnp.bfloat16)

    rows = in_inverse.shape[0]
    left = jnp.concatenate([in_inverse, gram_inverse], axis=0)
    both = add_columns(left, next_rows).astype(jnp.bfloat16)
    both_out = ring_product(both, out_inverse)
    precond = both_out[:rows]
    precond_image = both_out[rows:] + damping * precond
    inner_next, z_hz, z_hd, d_hz = global_sums(
        inner_part(residual, precond),
        inner_part(precond, precond_image),
        inner_part(precond, image),
        inner_part(direction, precond_image),
    )
    beta = inner_next / inner_now
    direction = precond + beta * direction
    image = precond_image + beta * image
    energy = z_hz + beta * (z_hd + d_hz) + beta * beta * energy
    alpha = inner_next / energy
    newton_step = newton_step + alpha * direction
    residual = residual - alpha * image
    return (newton_step, residual)


def solution(mesh):
    cores = 2
    split = jax.sharding.Mesh(
        mesh.devices.reshape(mesh.shape["fsdp"] // cores, cores, mesh.shape["fac"]),
        ("pairs", "core", "fac"),
    )
    placed = (
        P(FSDP, None),
        P(FSDP, "fac"),
        P(FSDP),
        P(FSDP),
        P(),
        P(FSDP, None),
        P(None, "fac"),
    )
    return jax.shard_map(
        body,
        mesh=split,
        in_specs=placed,
        out_specs=(P(FSDP, "fac"), P(FSDP, "fac")),
        check_vma=False,
    )
```

```python
import math

import jax
import jax.numpy as jnp
from jax import lax
from jax.experimental import pallas as pl
from jax.sharding import PartitionSpec as P

ITERS = 2


damping = 0.3


def add_columns(matrix, piece):
    return jnp.dot(matrix, piece, preferred_element_type=jnp.float32)


def transposed_term(matrix, right):
    return lax.dot_general(
        matrix, right, (((0,), (0,)), ((), ())), preferred_element_type=jnp.float32
    )


FSDP = ("pairs", "core")


def ring_product(piece, right):
    n = lax.axis_size("fac")
    me = lax.axis_index("fac")
    width = piece.shape[1]

    def right_block(k):
        return lax.dynamic_slice_in_dim(right, (k % n) * width, width, axis=0)

    total = add_columns(piece, right_block(me))
    ahead = piece
    behind = piece
    for step in range(1, n // 2 + 1):
        ahead = lax.ppermute(ahead, "fac", [(j, (j + 1) % n) for j in range(n)])
        total = total + add_columns(ahead, right_block(me - step))
        if 2 * step < n:
            behind = lax.ppermute(behind, "fac", [(j, (j - 1) % n) for j in range(n)])
            total = total + add_columns(behind, right_block(me + step))
    return total


def block_term(activations, right, factor, scale, own_half=None):
    pairs, cores = lax.axis_size("pairs"), lax.axis_size("core")
    tokens, d_in = activations.shape
    rows = d_in // (pairs * cores)
    cols = right.shape[1] if own_half is None else own_half[1]
    step = 384 if cols % 384 == 0 else cols

    def kernel(a_ref, x_ref, f_ref, o_ref):
        if own_half is None:
            x = x_ref[...]
        else:
            start = (lax.axis_index("fac") * 2 + own_half[0]) * cols + pl.program_id(0) * step
            x = a_ref[:, pl.ds(pl.multiple_of(start, 128), step)]
        scaled = (x.astype(jnp.float32) * f_ref[...].reshape(tokens, 1)).astype(jnp.bfloat16)
        product = lax.dot_general(
            a_ref[...], scaled, (((0,), (0,)), ((), ())), preferred_element_type=jnp.float32
        )
        product = (product * scale).astype(o_ref.dtype)
        for block in range(pairs * cores):
            o_ref[block % cores, block // cores] = product[block * rows : (block + 1) * rows]

    return pl.pallas_call(
        kernel,
        grid=(cols // step,),
        in_specs=[
            pl.BlockSpec((tokens, d_in), lambda j: (0, 0)),
            pl.BlockSpec((tokens, step), lambda j: (0, j if own_half is None else 0)),
            pl.BlockSpec((tokens,), lambda j: (0,)),
        ],
        out_specs=pl.BlockSpec((cores, pairs, rows, step), lambda j: (0, 0, 0, j)),
        out_shape=jax.ShapeDtypeStruct((cores, pairs, rows, cols), jnp.bfloat16),
    )(activations, right, factor)


def scatter_sum(blocks):
    cores = lax.axis_size("core")
    me = lax.axis_index("core")
    sibling = [(j, (j + 1) % cores) for j in range(cores)]
    sent = lax.ppermute(lax.dynamic_index_in_dim(blocks, 1 - me, 0, keepdims=False), "core", sibling)
    own = lax.dynamic_index_in_dim(blocks, me, 0, keepdims=False)
    chip_sum = (own.astype(jnp.float32) + sent.astype(jnp.float32)).astype(jnp.bfloat16)
    received = lax.all_to_all(chip_sum, "pairs", 0, 0, tiled=False)
    return lax.optimization_barrier(jnp.sum(received.astype(jnp.float32), axis=0))


def global_sums(*partials):
    devices = lax.axis_size("pairs") * lax.axis_size("core") * lax.axis_size("fac")
    stacked = jnp.broadcast_to(jnp.stack(partials)[None, :], (devices, len(partials)))
    received = lax.all_to_all(stacked, FSDP + ("fac",), 0, 0, tiled=True)
    total = jnp.sum(received, axis=0)
    return tuple(total[i] for i in range(len(partials)))


def body(activations, out_grads, token_ids, forget_mask, importance, in_inverse, out_inverse):
    tok_rows, d_in = activations.shape
    total = tok_rows * lax.axis_size("pairs") * lax.axis_size("core")
    keep = 1.0 - forget_mask.astype(jnp.float32)
    lanes = 128
    table_rows = importance.reshape(importance.shape[0] // lanes, lanes)[token_ids // lanes]
    lane_ids = lax.broadcasted_iota(jnp.int32, table_rows.shape, 1)
    picked = jnp.sum(
        jnp.where(lane_ids == (token_ids % lanes)[:, None], table_rows, 0.0), axis=1
    )
    weights = picked * keep / total
    grad_scale = 1.0 / math.sqrt(total)

    gradient = scatter_sum(
        block_term(activations, out_grads, forget_mask.astype(jnp.float32), grad_scale)
    )

    def gather_rows(matrix):
        return lax.all_gather(matrix.astype(jnp.bfloat16), FSDP, axis=0, tiled=True)

    def precondition(gathered):
        mixed = add_columns(in_inverse, gathered)
        mixed_low = mixed.astype(jnp.bfloat16)
        return jnp.dot(
            lax.all_gather(mixed_low, "fac", axis=1, tiled=True),
            out_inverse,
            preferred_element_type=jnp.float32,
        )

    def inner_part(left, right):
        return jnp.sum(left * right)

    d_out_part = out_inverse.shape[1]
    in_cols = lax.all_gather(
        lax.dynamic_slice_in_dim(in_inverse, lax.axis_index("fac") * d_out_part, d_out_part, axis=1),
        FSDP,
        axis=0,
        tiled=True,
    )

    gradient, in_cols = lax.optimization_barrier((gradient, in_cols))
    residual = -gradient
    residual_rows = gather_rows(residual)

    gram_cols = d_in // lax.axis_size("fac")
    half = gram_cols // 2
    gram_first = block_term(activations, activations, weights, 1.0, own_half=(0, half))
    gram_second = block_term(activations, activations, weights, 1.0, own_half=(1, half))
    residual_rows, first_rows = lax.optimization_barrier((residual_rows, scatter_sum(gram_first)))
    precond = precondition(residual_rows)
    gram_own = jnp.concatenate([first_rows, scatter_sum(gram_second)], axis=1)
    gram_rows = lax.all_gather(gram_own.astype(jnp.bfloat16), "fac", axis=1, tiled=True)

    def curvature(matrix):
        return add_columns(gram_rows, gather_rows(matrix)) + damping * matrix

    direction = precond
    image = curvature(direction)
    image_rows = gather_rows(image)
    inner_now, energy = global_sums(inner_part(residual, precond), inner_part(direction, image))
    gram_inverse = lax.all_gather(
        add_columns(gram_rows, in_cols).astype(jnp.bfloat16), "fac", axis=1, tiled=True
    )
    alpha = inner_now / energy
    newton_step = alpha * direction
    residual = residual - alpha * image
    next_rows = (
        residual_rows.astype(jnp.float32) - alpha * image_rows.astype(jnp.float32)
    ).astype(jnp.bfloat16)

    rows = in_inverse.shape[0]
    left = jnp.concatenate([in_inverse, gram_inverse], axis=0)
    both = add_columns(left, next_rows).astype(jnp.bfloat16)
    both_out = ring_product(both, out_inverse)
    precond = both_out[:rows]
    precond_image = both_out[rows:] + damping * precond
    inner_next, z_hz, z_hd, d_hz = global_sums(
        inner_part(residual, precond),
        inner_part(precond, precond_image),
        inner_part(precond, image),
        inner_part(direction, precond_image),
    )
    beta = inner_next / inner_now
    direction = precond + beta * direction
    image = precond_image + beta * image
    energy = z_hz + beta * (z_hd + d_hz) + beta * beta * energy
    alpha = inner_next / energy
    newton_step = newton_step + alpha * direction
    residual = residual - alpha * image
    return (newton_step, residual)


def solution(mesh):
    cores = 2
    split = jax.sharding.Mesh(
        mesh.devices.reshape(mesh.shape["fsdp"] // cores, cores, mesh.shape["fac"]),
        ("pairs", "core", "fac"),
    )
    placed = (
        P(FSDP, None),
        P(FSDP, "fac"),
        P(FSDP),
        P(FSDP),
        P(),
        P(FSDP, None),
        P(None, "fac"),
    )
    return jax.shard_map(
        body,
        mesh=split,
        in_specs=placed,
        out_specs=(P(FSDP, "fac"), P(FSDP, "fac")),
        check_vma=False,
    )
```

```python
import math

import jax
import jax.numpy as jnp
from jax import lax
from jax.experimental import pallas as pl
from jax.sharding import PartitionSpec as P

ITERS = 2


damping = 0.3


def add_columns(matrix, piece):
    return jnp.dot(matrix, piece, preferred_element_type=jnp.float32)


def transposed_term(matrix, right):
    return lax.dot_general(
        matrix, right, (((0,), (0,)), ((), ())), preferred_element_type=jnp.float32
    )


FSDP = ("pairs", "core")


def ring_product(piece, right):
    n = lax.axis_size("fac")
    me = lax.axis_index("fac")
    width = piece.shape[1]

    def right_block(k):
        return lax.dynamic_slice_in_dim(right, (k % n) * width, width, axis=0)

    total = add_columns(piece, right_block(me))
    ahead = piece
    behind = piece
    for step in range(1, n // 2 + 1):
        ahead = lax.ppermute(ahead, "fac", [(j, (j + 1) % n) for j in range(n)])
        total = total + add_columns(ahead, right_block(me - step))
        if 2 * step < n:
            behind = lax.ppermute(behind, "fac", [(j, (j - 1) % n) for j in range(n)])
            total = total + add_columns(behind, right_block(me + step))
    return total


def block_term(activations, right, factor, scale, own_half=None):
    pairs, cores = lax.axis_size("pairs"), lax.axis_size("core")
    tokens, d_in = activations.shape
    rows = d_in // (pairs * cores)
    cols = right.shape[1] if own_half is None else own_half[1]
    step = cols

    def kernel(a_ref, x_ref, f_ref, o_ref):
        if own_half is None:
            x = x_ref[...]
        else:
            start = (lax.axis_index("fac") * 2 + own_half[0]) * cols + pl.program_id(0) * step
            x = a_ref[:, pl.ds(pl.multiple_of(start, 128), step)]
        scaled = (x.astype(jnp.float32) * f_ref[...].reshape(tokens, 1)).astype(jnp.bfloat16)
        product = lax.dot_general(
            a_ref[...], scaled, (((0,), (0,)), ((), ())), preferred_element_type=jnp.float32
        )
        product = (product * scale).astype(o_ref.dtype)
        for block in range(pairs * cores):
            o_ref[block % cores, block // cores] = product[block * rows : (block + 1) * rows]

    return pl.pallas_call(
        kernel,
        grid=(cols // step,),
        in_specs=[
            pl.BlockSpec((tokens, d_in), lambda j: (0, 0)),
            pl.BlockSpec((tokens, step), lambda j: (0, j if own_half is None else 0)),
            pl.BlockSpec((tokens,), lambda j: (0,)),
        ],
        out_specs=pl.BlockSpec((cores, pairs, rows, step), lambda j: (0, 0, 0, j)),
        out_shape=jax.ShapeDtypeStruct((cores, pairs, rows, cols), jnp.bfloat16),
    )(activations, right, factor)


def scatter_sum(blocks):
    cores = lax.axis_size("core")
    me = lax.axis_index("core")
    sibling = [(j, (j + 1) % cores) for j in range(cores)]
    sent = lax.ppermute(lax.dynamic_index_in_dim(blocks, 1 - me, 0, keepdims=False), "core", sibling)
    own = lax.dynamic_index_in_dim(blocks, me, 0, keepdims=False)
    chip_sum = (own.astype(jnp.float32) + sent.astype(jnp.float32)).astype(jnp.bfloat16)
    received = lax.all_to_all(chip_sum, "pairs", 0, 0, tiled=False)
    return lax.optimization_barrier(jnp.sum(received.astype(jnp.float32), axis=0))


def global_sums(*partials):
    devices = lax.axis_size("pairs") * lax.axis_size("core") * lax.axis_size("fac")
    stacked = jnp.broadcast_to(jnp.stack(partials)[None, :], (devices, len(partials)))
    received = lax.all_to_all(stacked, FSDP + ("fac",), 0, 0, tiled=True)
    total = jnp.sum(received, axis=0)
    return tuple(total[i] for i in range(len(partials)))


def body(activations, out_grads, token_ids, forget_mask, importance, in_inverse, out_inverse):
    tok_rows, d_in = activations.shape
    total = tok_rows * lax.axis_size("pairs") * lax.axis_size("core")
    keep = 1.0 - forget_mask.astype(jnp.float32)
    lanes = 128
    table_rows = importance.reshape(importance.shape[0] // lanes, lanes)[token_ids // lanes]
    lane_ids = lax.broadcasted_iota(jnp.int32, table_rows.shape, 1)
    picked = jnp.sum(
        jnp.where(lane_ids == (token_ids % lanes)[:, None], table_rows, 0.0), axis=1
    )
    weights = picked * keep / total
    grad_scale = 1.0 / math.sqrt(total)

    gradient = scatter_sum(
        block_term(activations, out_grads, forget_mask.astype(jnp.float32), grad_scale)
    )

    def gather_rows(matrix):
        return lax.all_gather(matrix.astype(jnp.bfloat16), FSDP, axis=0, tiled=True)

    def precondition(gathered):
        mixed = add_columns(in_inverse, gathered)
        mixed_low = mixed.astype(jnp.bfloat16)
        return jnp.dot(
            lax.all_gather(mixed_low, "fac", axis=1, tiled=True),
            out_inverse,
            preferred_element_type=jnp.float32,
        )

    def inner_part(left, right):
        return jnp.sum(left * right)

    d_out_part = out_inverse.shape[1]
    in_cols = lax.all_gather(
        lax.dynamic_slice_in_dim(in_inverse, lax.axis_index("fac") * d_out_part, d_out_part, axis=1),
        FSDP,
        axis=0,
        tiled=True,
    )

    gradient, in_cols = lax.optimization_barrier((gradient, in_cols))
    residual = -gradient
    residual_rows = gather_rows(residual)

    gram_cols = d_in // lax.axis_size("fac")
    half = gram_cols // 2
    gram_first = block_term(activations, activations, weights, 1.0, own_half=(0, half))
    gram_second = block_term(activations, activations, weights, 1.0, own_half=(1, half))
    residual_rows, first_rows = lax.optimization_barrier((residual_rows, scatter_sum(gram_first)))
    precond = precondition(residual_rows)
    gram_own = jnp.concatenate([first_rows, scatter_sum(gram_second)], axis=1)
    gram_rows = lax.all_gather(gram_own.astype(jnp.bfloat16), "fac", axis=1, tiled=True)

    def curvature(matrix):
        return add_columns(gram_rows, gather_rows(matrix)) + damping * matrix

    direction = precond
    image = curvature(direction)
    image_rows = gather_rows(image)
    inner_now, energy = global_sums(inner_part(residual, precond), inner_part(direction, image))
    gram_inverse = lax.all_gather(
        add_columns(gram_rows, in_cols).astype(jnp.bfloat16), "fac", axis=1, tiled=True
    )
    alpha = inner_now / energy
    newton_step = alpha * direction
    residual = residual - alpha * image
    next_rows = (
        residual_rows.astype(jnp.float32) - alpha * image_rows.astype(jnp.float32)
    ).astype(jnp.bfloat16)

    rows = in_inverse.shape[0]
    left = jnp.concatenate([in_inverse, gram_inverse], axis=0)
    both = add_columns(left, next_rows).astype(jnp.bfloat16)
    both_out = ring_product(both, out_inverse)
    precond = both_out[:rows]
    precond_image = both_out[rows:] + damping * precond
    inner_next, z_hz, z_hd, d_hz = global_sums(
        inner_part(residual, precond),
        inner_part(precond, precond_image),
        inner_part(precond, image),
        inner_part(direction, precond_image),
    )
    beta = inner_next / inner_now
    direction = precond + beta * direction
    image = precond_image + beta * image
    energy = z_hz + beta * (z_hd + d_hz) + beta * beta * energy
    alpha = inner_next / energy
    newton_step = newton_step + alpha * direction
    residual = residual - alpha * image
    return (newton_step, residual)


def solution(mesh):
    cores = 2
    split = jax.sharding.Mesh(
        mesh.devices.reshape(mesh.shape["fsdp"] // cores, cores, mesh.shape["fac"]),
        ("pairs", "core", "fac"),
    )
    placed = (
        P(FSDP, None),
        P(FSDP, "fac"),
        P(FSDP),
        P(FSDP),
        P(),
        P(FSDP, None),
        P(None, "fac"),
    )
    return jax.shard_map(
        body,
        mesh=split,
        in_specs=placed,
        out_specs=(P(FSDP, "fac"), P(FSDP, "fac")),
        check_vma=False,
    )
```
